256 devices in a mesh: geo: 8 (over x, core), curve: 32 (over y, z).
Axes of the slice: x: 4, y: 4, z: 8, core: 2. Of those that a mesh axis runs over, the one named last changes fastest.
Arguments:
- tokens: bfloat16 [262144, 512], P(('geo', 'curve')), parts along dimension 0, may hold values from -80 to 80
- w_query: bfloat16 [512, 512], replicated, may hold values from -0.25 to 0.25
- w_keyval: bfloat16 [512, 1024], replicated, may hold values from -0.25 to 0.25
- w_out: bfloat16 [512, 512], replicated, may hold values from -0.25 to 0.25
- block_list: int32 [2048, 12], P(('geo', 'curve')), parts along dimension 0, may hold values from 0 to 255, as said below
- block_count: int32 [2048], P(('geo', 'curve')), parts along dimension 0, may hold values from 2 to 12, as said below
- bnd_ids: int32 [4096], P('geo'), parts along dimension 0, may hold values from 0 to 32767, as said below
Outputs:
- mixed: bfloat16 [262144, 512], P(('geo', 'curve')), parts along dimension 0
The draws below stay inside these ranges and needn't reach their ends.
There are 8 independent parts, one for each index of `geo`. The reference program is written for one: setup_inputs(seed, part) draws one part's arguments, and reference() takes and returns one part's arrays. A program takes and returns all parts, laid end to end along the dimension named above; an argument that names none is the same for every part. Nothing has to cross between parts.
Inputs may be any that keep to these rules, and one draw needn't show every extreme that they name: `block_list`: entry 0 of row b is b itself; the other entries of a row are distinct blocks other than b whose owners lie at most two devices of curve away from b's owner (device index = block // 8); entries at or past block_count[b] are not used. `block_count`: it equals 12 on the first block of every device. `bnd_ids`: Distinct; listed in increasing order of owner id // 1024; exactly eight owners hold 128, 128, 96, 64, 48, 24, 16 and 8 of them, the other devices none.
All inputs are finite; a program needn't handle non-finite values.
Results may differ from the reference program's by a relative error of at most 0.012.
The reference program's roundings to bfloat16 on the way (of `queries`, `keyvals`, `weights` and `context`) count: a program that leaves them out, or rounds other values in their place, can miss the bound.
Values may be sent and summed in bfloat16 or wider, within the bound.
No kernel may reach another device: no remote copies, remote signals or barrier semaphores. Data moves between devices by JAX's collectives and lax.ppermute only.
A program may use at most 128 MiB of HBM per device.

```python
import jax
import jax.numpy as jnp
from jax import lax

D = 512
HEADS = 8
BLOCK = 128
NB = 12
TOK_DEV = 1024
BCAP = 128
NBD = 512
TOKENS = 32768
N_CURVE = 32


def draw_tokens(key, part):
    base = jnp.clip(jax.random.normal(key, (TOKENS, D), jnp.float32), -5.5, 5.5)
    return base.astype(jnp.bfloat16)


def draw_block_list(key, part):
    nblk = TOKENS // BLOCK
    per_dev = TOK_DEV // BLOCK
    span = 5 * per_dev
    query = jnp.arange(nblk, dtype=jnp.int32)
    shard = query // per_dev
    low = jnp.maximum(shard - 2, 0) * per_dev
    high = jnp.minimum(shard + 3, N_CURVE) * per_dev
    cand = low[:, None] + jnp.arange(span, dtype=jnp.int32)[None, :]
    usable = (cand < high[:, None]) & (cand != query[:, None])
    noise = jax.random.randint(key, (nblk, span), 0, 1 << 20)
    score = jnp.where(usable, noise, 1 << 21) * 64 + jnp.arange(span, dtype=jnp.int32)[None, :]
    order = jnp.argsort(score, axis=1)
    chosen = jnp.take_along_axis(cand, order[:, :NB - 1], axis=1)
    return jnp.concatenate([query[:, None], chosen], axis=1).astype(jnp.int32)


def draw_block_count(key, part):
    nblk = TOKENS // BLOCK
    per_dev = TOK_DEV // BLOCK
    query = jnp.arange(nblk, dtype=jnp.int32)
    drawn = jax.random.randint(key, (nblk,), 2, NB + 1)
    return jnp.where(query % per_dev == 0, NB, drawn).astype(jnp.int32)


def draw_bnd_ids(key, part):
    inner = jax.random.fold_in(key, 77)
    owners = jax.random.permutation(jax.random.fold_in(inner, 1), N_CURVE)[:8]
    shares = jnp.array([16, 16, 12, 8, 6, 3, 2, 1], jnp.int32) * (BCAP // 16)
    counts = jnp.zeros((N_CURVE,), jnp.int32).at[owners].set(shares)
    shard_ids = jnp.arange(N_CURVE, dtype=jnp.int32)
    spots = jax.vmap(lambda r: jax.random.permutation(jax.random.fold_in(inner, 100 + r), TOK_DEV)[:BCAP])(shard_ids)
    glob = shard_ids[:, None] * TOK_DEV + spots.astype(jnp.int32)
    valid = jnp.arange(BCAP, dtype=jnp.int32)[None, :] < counts[:, None]
    flat = jnp.arange(N_CURVE * BCAP, dtype=jnp.int32).reshape(N_CURVE, BCAP)
    score = jnp.where(valid, flat, N_CURVE * BCAP + flat).reshape(-1)
    order = jnp.argsort(score)[:NBD]
    return glob.reshape(-1)[order].astype(jnp.int32)


def centred(rng, extent, spread, limit, held_as=jnp.bfloat16):
    entries = jax.random.normal(rng, extent, jnp.float32) * spread
    return jnp.minimum(jnp.maximum(entries, -limit), limit).astype(held_as)


def setup_inputs(seed: int = 0, part: int = 0) -> dict:
    streams_of = jax.random.split(jax.random.key(seed), 8)
    own_keys = jax.random.split(jax.random.fold_in(streams_of[7], part), 8)
    return {
        "tokens": draw_tokens(jax.random.fold_in(jax.random.fold_in(streams_of[7], part), 71), part),
        "w_query": centred(streams_of[1], (D, D), D ** -0.5, 0.25),
        "w_keyval": centred(streams_of[2], (D, 2 * D), D ** -0.5, 0.25),
        "w_out": centred(streams_of[3], (D, D), D ** -0.5, 0.25),
        "block_list": draw_block_list(jax.random.fold_in(jax.random.fold_in(streams_of[7], part), 71), part),
        "block_count": draw_block_count(jax.random.fold_in(jax.random.fold_in(streams_of[7], part), 71), part),
        "bnd_ids": draw_bnd_ids(jax.random.fold_in(jax.random.fold_in(streams_of[7], part), 71), part),
    }


def attend_group(query, keyvals_near, live, bnd_kv):
    width = D
    head_dim = D // HEADS
    groups = query.shape[0]
    scale = 1.0 / (head_dim ** 0.5)
    qh = query.reshape(groups, BLOCK, HEADS, head_dim).astype(jnp.float32)
    keys = keyvals_near[..., :width].reshape(groups, -1, HEADS, head_dim).astype(jnp.float32)
    vals = keyvals_near[..., width:].reshape(groups, -1, HEADS, head_dim).astype(jnp.float32)
    bkeys = bnd_kv[:, :width].reshape(-1, HEADS, head_dim).astype(jnp.float32)
    bvals = bnd_kv[:, width:].reshape(-1, HEADS, head_dim).astype(jnp.float32)
    near_scores = jnp.einsum('gqhd,gkhd->ghqk', qh, keys) * scale
    near_scores = jnp.where(live[:, None, None, :], near_scores, -1e30)
    far_scores = jnp.einsum('gqhd,khd->ghqk', qh, bkeys) * scale
    scores = jnp.concatenate([near_scores, far_scores], axis=-1)
    top = jnp.max(scores, axis=-1, keepdims=True)
    expo = jnp.exp(scores - top)
    weights = (expo / jnp.sum(expo, axis=-1, keepdims=True)).astype(jnp.bfloat16).astype(jnp.float32)
    span = keys.shape[1]
    ctx = jnp.einsum('ghqk,gkhd->gqhd', weights[..., :span], vals)
    ctx = ctx + jnp.einsum('ghqk,khd->gqhd', weights[..., span:], bvals)
    return ctx.reshape(groups * BLOCK, width).astype(jnp.bfloat16)


def reference(tokens, w_query, w_keyval, w_out, block_list, block_count, bnd_ids):
    queries = jnp.dot(tokens, w_query, preferred_element_type=jnp.float32).astype(jnp.bfloat16)
    keyvals = jnp.dot(tokens, w_keyval, preferred_element_type=jnp.float32).astype(jnp.bfloat16)
    bnd_kv = jnp.take(keyvals, bnd_ids.astype(jnp.int32), axis=0)
    nblk = TOKENS // BLOCK
    q_groups = queries.reshape(nblk // 2, 2, BLOCK, D)
    lists = block_list.astype(jnp.int32).reshape(nblk // 2, 2, NB)
    counts = block_count.astype(jnp.int32).reshape(nblk // 2, 2)

    def step(item):
        query, blocks, count = item
        rows = (blocks[:, :, None] * BLOCK + jnp.arange(BLOCK, dtype=jnp.int32)).reshape(2, NB * BLOCK)
        picked = jnp.take(keyvals, rows, axis=0)
        live = (jnp.arange(NB * BLOCK, dtype=jnp.int32) // BLOCK)[None, :] < count[:, None]
        return attend_group(query, picked, live, bnd_kv)

    context = lax.map(step, (q_groups, lists, counts)).reshape(TOKENS, D)
    return jnp.dot(context, w_out, preferred_element_type=jnp.float32).astype(jnp.bfloat16)
```

```python
import jax
import jax.numpy as jnp
from jax import lax
from jax.sharding import PartitionSpec as P

HEADS = 8
BLOCK = 128
NB = 12
BCAP = 128


def from_behind(value, axis, steps):
    count = lax.axis_size(axis)
    first, last = (max(0, -steps), min(count, count - steps))
    return lax.ppermute(value, axis, [(source, source + steps) for source in range(first, last)])


def head_major(rows, w_keyval, width):
    head_dim = width // HEADS
    weight = w_keyval.reshape(width, 2 * HEADS, head_dim)
    return jnp.einsum("td,dhe->hte", rows, weight, preferred_element_type=jnp.float32).astype(
        jnp.bfloat16
    )


def on_device(tokens, w_query, w_keyval, w_out, block_list, block_count, bnd_ids):
    tok_dev, width = tokens.shape
    head_dim = width // HEADS
    nblocks = tok_dev // BLOCK
    npairs = nblocks // 2
    nbound = bnd_ids.shape[0]
    scale = 1.0 / head_dim**0.5
    member = lax.axis_index("curve")
    query_w = w_query.reshape(width, HEADS, head_dim)
    queries = jnp.einsum(
        "gbtd,dhe->ghbte",
        tokens.reshape(npairs, 2, BLOCK, width),
        query_w,
        preferred_element_type=jnp.float32,
    ).astype(jnp.bfloat16)
    pieces = []
    for offset in (-2, -1, 0, 1, 2):
        if offset == 0:
            pieces.append(tokens)
        else:
            pieces.append(from_behind(tokens, "curve", -offset))
    nearby = head_major(jnp.concatenate(pieces, axis=0), w_keyval, width)
    nearby = nearby.reshape(2 * HEADS, 5 * nblocks, BLOCK, head_dim)
    owner = bnd_ids // tok_dev
    local_pos = jnp.clip(bnd_ids - member * tok_dev, 0, tok_dev - 1)
    mine = owner == member
    rows = jnp.where(mine[:, None], jnp.take(tokens, local_pos, axis=0), jnp.zeros((), tokens.dtype))
    gathered = lax.psum(rows, "curve")
    bnd_kv = head_major(gathered, w_keyval, width)
    bkeys = bnd_kv[:HEADS]
    bvals = bnd_kv[HEADS:]
    first_block = (member - 2) * nblocks
    lists = (block_list - first_block).reshape(npairs, 2, NB)
    counts = block_count.reshape(npairs, 2)

    def attend(item):
        query, relative, count = item
        picked = jnp.take(nearby, relative.reshape(2 * NB), axis=1)
        picked = picked.reshape(2 * HEADS, 2, NB * BLOCK, head_dim)
        keys = picked[:HEADS]
        vals = picked[HEADS:]
        live = (jnp.arange(NB * BLOCK, dtype=jnp.int32) // BLOCK)[None, :] < count[:, None]
        near_scores = (
            jnp.einsum("hgqd,hgkd->hgqk", query, keys, preferred_element_type=jnp.float32) * scale
        )
        near_scores = jnp.where(live[None, :, None, :], near_scores, -1e30)
        far_scores = (
            jnp.einsum("hgqd,hkd->hgqk", query, bkeys, preferred_element_type=jnp.float32) * scale
        )
        top = jnp.maximum(
            jnp.max(near_scores, axis=-1, keepdims=True),
            jnp.max(far_scores, axis=-1, keepdims=True),
        )
        near_exp = jnp.exp(near_scores - top)
        far_exp = jnp.exp(far_scores - top)
        total = jnp.sum(near_exp, axis=-1, keepdims=True) + jnp.sum(far_exp, axis=-1, keepdims=True)
        near_w = (near_exp / total).astype(jnp.bfloat16)
        far_w = (far_exp / total).astype(jnp.bfloat16)
        ctx = jnp.einsum("hgqk,hgkd->hgqd", near_w, vals, preferred_element_type=jnp.float32)
        ctx = ctx + jnp.einsum("hgqk,hkd->hgqd", far_w, bvals, preferred_element_type=jnp.float32)
        return ctx.astype(jnp.bfloat16)

    context = lax.map(attend, (queries, lists, counts))
    out_w = w_out.reshape(HEADS, head_dim, width)
    mixed = jnp.einsum("phgqd,hde->pgqe", context, out_w, preferred_element_type=jnp.float32)
    return mixed.reshape(tok_dev, width).astype(jnp.bfloat16)


def solution(mesh):
    in_specs = (
        P(("geo", "curve"), None),
        P(),
        P(),
        P(),
        P(("geo", "curve"), None),
        P(("geo", "curve")),
        P("geo"),
    )
    out_specs = P(("geo", "curve"), None)
    return jax.shard_map(
        on_device, mesh=mesh, in_specs=in_specs, out_specs=out_specs, check_vma=False
    )
```

```python
import jax
import jax.numpy as jnp
from jax import lax
from jax.sharding import PartitionSpec as P

HEADS = 8
BLOCK = 128
NB = 12
BCAP = 128


def from_behind(value, axis, steps):
    count = lax.axis_size(axis)
    first, last = (max(0, -steps), min(count, count - steps))
    return lax.ppermute(value, axis, [(source, source + steps) for source in range(first, last)])


def share_rows(rows, owner, member):
    count = lax.axis_size("curve")
    span = 1
    while span < count:
        pairs = [(source, source ^ span) for source in range(count) if source ^ span < count]
        other = lax.ppermute(rows, "curve", pairs)
        theirs = (owner // span) == ((member // span) ^ 1)
        rows = jnp.where(theirs[:, None], other, rows)
        span *= 2
    return rows


def head_major(rows, w_keyval, width):
    head_dim = width // HEADS
    weight = w_keyval.reshape(width, 2 * HEADS, head_dim)
    return jnp.einsum("td,dhe->hte", rows, weight, preferred_element_type=jnp.float32).astype(
        jnp.bfloat16
    )


def on_device(tokens, w_query, w_keyval, w_out, block_list, block_count, bnd_ids):
    tok_dev, width = tokens.shape
    head_dim = width // HEADS
    nblocks = tok_dev // BLOCK
    npairs = nblocks // 2
    nbound = bnd_ids.shape[0]
    scale = 1.0 / head_dim**0.5
    member = lax.axis_index("curve")
    query_w = w_query.reshape(width, HEADS, head_dim)
    queries = jnp.einsum(
        "gbtd,dhe->ghbte",
        tokens.reshape(npairs, 2, BLOCK, width),
        query_w,
        preferred_element_type=jnp.float32,
    ).astype(jnp.bfloat16)
    pieces = []
    for offset in (-2, -1, 0, 1, 2):
        if offset == 0:
            pieces.append(tokens)
        else:
            pieces.append(from_behind(tokens, "curve", -offset))
    nearby = head_major(jnp.concatenate(pieces, axis=0), w_keyval, width)
    nearby = nearby.reshape(2 * HEADS, 5 * nblocks, BLOCK, head_dim)
    owner = bnd_ids // tok_dev
    local_pos = jnp.clip(bnd_ids - member * tok_dev, 0, tok_dev - 1)
    mine = owner == member
    rows = jnp.where(mine[:, None], jnp.take(tokens, local_pos, axis=0), jnp.zeros((), tokens.dtype))
    gathered = share_rows(rows, owner, member)
    bnd_kv = head_major(gathered, w_keyval, width)
    bkeys = bnd_kv[:HEADS]
    bvals = bnd_kv[HEADS:]
    first_block = (member - 2) * nblocks
    lists = (block_list - first_block).reshape(npairs, 2, NB)
    counts = block_count.reshape(npairs, 2)

    def attend(item):
        query, relative, count = item
        picked = jnp.take(nearby, relative.reshape(2 * NB), axis=1)
        picked = picked.reshape(2 * HEADS, 2, NB * BLOCK, head_dim)
        keys = picked[:HEADS]
        vals = picked[HEADS:]
        live = (jnp.arange(NB * BLOCK, dtype=jnp.int32) // BLOCK)[None, :] < count[:, None]
        near_scores = (
            jnp.einsum("hgqd,hgkd->hgqk", query, keys, preferred_element_type=jnp.float32) * scale
        )
        near_scores = jnp.where(live[None, :, None, :], near_scores, -1e30)
        far_scores = (
            jnp.einsum("hgqd,hkd->hgqk", query, bkeys, preferred_element_type=jnp.float32) * scale
        )
        top = jnp.maximum(
            jnp.max(near_scores, axis=-1, keepdims=True),
            jnp.max(far_scores, axis=-1, keepdims=True),
        )
        near_exp = jnp.exp(near_scores - top)
        far_exp = jnp.exp(far_scores - top)
        total = jnp.sum(near_exp, axis=-1, keepdims=True) + jnp.sum(far_exp, axis=-1, keepdims=True)
        near_w = (near_exp / total).astype(jnp.bfloat16)
        far_w = (far_exp / total).astype(jnp.bfloat16)
        ctx = jnp.einsum("hgqk,hgkd->hgqd", near_w, vals, preferred_element_type=jnp.float32)
        ctx = ctx + jnp.einsum("hgqk,hkd->hgqd", far_w, bvals, preferred_element_type=jnp.float32)
        return ctx.astype(jnp.bfloat16)

    context = lax.map(attend, (queries, lists, counts))
    out_w = w_out.reshape(HEADS, head_dim, width)
    mixed = jnp.einsum("phgqd,hde->pgqe", context, out_w, preferred_element_type=jnp.float32)
    return mixed.reshape(tok_dev, width).astype(jnp.bfloat16)


def solution(mesh):
    in_specs = (
        P(("geo", "curve"), None),
        P(),
        P(),
        P(),
        P(("geo", "curve"), None),
        P(("geo", "curve")),
        P("geo"),
    )
    out_specs = P(("geo", "curve"), None)
    return jax.shard_map(
        on_device, mesh=mesh, in_specs=in_specs, out_specs=out_specs, check_vma=False
    )
```

```python
import jax
import jax.numpy as jnp
from jax import lax
from jax.experimental import pallas as pl
from jax.experimental.pallas import tpu as pltpu
from jax.sharding import PartitionSpec as P

HEADS = 8
BLOCK = 128
NB = 12
BCAP = 128


def from_behind(value, axis, steps):
    count = lax.axis_size(axis)
    first, last = (max(0, -steps), min(count, count - steps))
    return lax.ppermute(value, axis, [(source, source + steps) for source in range(first, last)])


def share_rows(rows, owner, member):
    count = lax.axis_size("curve")
    span = 1
    while span < count:
        pairs = [(source, source ^ span) for source in range(count) if source ^ span < count]
        other = lax.ppermute(rows, "curve", pairs)
        theirs = (owner // span) == ((member // span) ^ 1)
        rows = jnp.where(theirs[:, None], other, rows)
        span *= 2
    return rows


def attention_kernel(rel_ref, cnt_ref, q_ref, kt_ref, vt_ref, bkt_ref, bvt_ref, o_ref):
    b = pl.program_id(0)
    count = cnt_ref[b]
    picks = [rel_ref[b * NB + i] for i in range(NB)]
    width = NB * BLOCK + bkt_ref.shape[2]
    lane = lax.broadcasted_iota(jnp.int32, (1, width), 1)
    live = (lane // BLOCK < count) | (lane >= NB * BLOCK)
    scale = 1.0 / q_ref.shape[3] ** 0.5
    for h in range(HEADS):
        query = q_ref[0, h]
        keys = jnp.concatenate([kt_ref[p, h] for p in picks] + [bkt_ref[h]], axis=1)
        scores = jnp.dot(query, keys, preferred_element_type=jnp.float32) * scale
        scores = jnp.where(live, scores, -1e30)
        top = jnp.max(scores, axis=1, keepdims=True)
        expo = jnp.exp(scores - top)
        total = jnp.sum(expo, axis=1, keepdims=True)
        weights = (expo / total).astype(jnp.bfloat16)
        values = jnp.concatenate([vt_ref[p, h] for p in picks] + [bvt_ref[h]], axis=1)
        ctx = lax.dot_general(
            values, weights, (((1,), (1,)), ((), ())), preferred_element_type=jnp.float32
        )
        o_ref[0, h] = ctx.astype(jnp.bfloat16)


def attention(rel, counts, q, kt, vt, bkt, bvt):
    nq = q.shape[0]
    nkb = kt.shape[0]
    head_dim = q.shape[3]
    nbound = bkt.shape[2]
    grid_spec = pltpu.PrefetchScalarGridSpec(
        num_scalar_prefetch=2,
        grid=(nq,),
        in_specs=[
            pl.BlockSpec((1, HEADS, BLOCK, head_dim), lambda b, r, c: (b, 0, 0, 0)),
            pl.BlockSpec((nkb, HEADS, head_dim, BLOCK), lambda b, r, c: (0, 0, 0, 0)),
            pl.BlockSpec((nkb, HEADS, head_dim, BLOCK), lambda b, r, c: (0, 0, 0, 0)),
            pl.BlockSpec((HEADS, head_dim, nbound), lambda b, r, c: (0, 0, 0)),
            pl.BlockSpec((HEADS, head_dim, nbound), lambda b, r, c: (0, 0, 0)),
        ],
        out_specs=pl.BlockSpec((1, HEADS, head_dim, BLOCK), lambda b, r, c: (b, 0, 0, 0)),
    )
    return pl.pallas_call(
        attention_kernel,
        grid_spec=grid_spec,
        out_shape=jax.ShapeDtypeStruct((nq, HEADS, head_dim, BLOCK), jnp.bfloat16),
    )(rel, counts, q, kt, vt, bkt, bvt)


def key_tiles(keyvals, width, head_dim):
    rows = keyvals.shape[0]
    keys = keyvals[:, :width].reshape(rows // BLOCK, BLOCK, HEADS, head_dim)
    vals = keyvals[:, width:].reshape(rows // BLOCK, BLOCK, HEADS, head_dim)
    return keys.transpose(0, 2, 3, 1), vals.transpose(0, 2, 3, 1)


def on_device(tokens, w_query, w_keyval, w_out, block_list, block_count, bnd_ids):
    tok_dev, width = tokens.shape
    head_dim = width // HEADS
    nblocks = tok_dev // BLOCK
    member = lax.axis_index("curve")
    queries = jnp.dot(tokens, w_query, preferred_element_type=jnp.float32).astype(jnp.bfloat16)
    queries = queries.reshape(nblocks, BLOCK, HEADS, head_dim).transpose(0, 2, 1, 3)
    pieces = []
    for offset in (-2, -1, 0, 1, 2):
        if offset == 0:
            pieces.append(tokens)
        else:
            pieces.append(from_behind(tokens, "curve", -offset))
    nearby = jnp.dot(
        jnp.concatenate(pieces, axis=0), w_keyval, preferred_element_type=jnp.float32
    ).astype(jnp.bfloat16)
    kt, vt = key_tiles(nearby, width, head_dim)
    owner = bnd_ids // tok_dev
    local_pos = jnp.clip(bnd_ids - member * tok_dev, 0, tok_dev - 1)
    mine = owner == member
    rows = jnp.where(mine[:, None], jnp.take(tokens, local_pos, axis=0), jnp.zeros((), tokens.dtype))
    gathered = share_rows(rows, owner, member)
    bnd_kv = jnp.dot(gathered, w_keyval, preferred_element_type=jnp.float32).astype(jnp.bfloat16)
    bkt, bvt = key_tiles(bnd_kv, width, head_dim)
    bkt = bkt.transpose(1, 2, 0, 3).reshape(HEADS, head_dim, -1)
    bvt = bvt.transpose(1, 2, 0, 3).reshape(HEADS, head_dim, -1)
    first_block = (member - 2) * nblocks
    rel = jnp.clip(block_list - first_block, 0, 5 * nblocks - 1).reshape(-1).astype(jnp.int32)
    context = attention(rel, block_count.astype(jnp.int32), queries, kt, vt, bkt, bvt)
    out_w = w_out.reshape(HEADS, head_dim, width)
    mixed = jnp.einsum("bhdt,hde->bte", context, out_w, preferred_element_type=jnp.float32)
    return mixed.reshape(tok_dev, width).astype(jnp.bfloat16)


def solution(mesh):
    in_specs = (
        P(("geo", "curve"), None),
        P(),
        P(),
        P(),
        P(("geo", "curve"), None),
        P(("geo", "curve")),
        P("geo"),
    )
    out_specs = P(("geo", "curve"), None)
    return jax.shard_map(
        on_device, mesh=mesh, in_specs=in_specs, out_specs=out_specs, check_vma=False
    )
```

```python
import jax
import jax.numpy as jnp
from jax import lax
from jax.experimental import pallas as pl
from jax.experimental.pallas import tpu as pltpu
from jax.sharding import PartitionSpec as P

HEADS = 8
BLOCK = 128
NB = 12
BCAP = 128


def from_behind(value, axis, steps):
    count = lax.axis_size(axis)
    first, last = (max(0, -steps), min(count, count - steps))
    return lax.ppermute(value, axis, [(source, source + steps) for source in range(first, last)])


def share_rows(rows, owner, member):
    count = lax.axis_size("curve")
    span = 1
    while span < count:
        pairs = [(source, source ^ span) for source in range(count) if source ^ span < count]
        other = lax.ppermute(rows, "curve", pairs)
        theirs = (owner // span) == ((member // span) ^ 1)
        rows = jnp.where(theirs[:, None], other, rows)
        span *= 2
    return rows


def attention_kernel(rel_ref, cnt_ref, q_ref, kvt_ref, bkt_ref, bvt_ref, o_ref):
    b = pl.program_id(0)
    count = cnt_ref[b]
    picks = [rel_ref[b * NB + i] for i in range(NB)]
    width = NB * BLOCK + bkt_ref.shape[2]
    lane = lax.broadcasted_iota(jnp.int32, (1, width), 1)
    live = (lane // BLOCK < count) | (lane >= NB * BLOCK)
    scale = 1.0 / q_ref.shape[3] ** 0.5
    for h in range(HEADS):
        query = q_ref[0, h]
        keys = jnp.concatenate([kvt_ref[p, h] for p in picks] + [bkt_ref[h]], axis=1)
        scores = jnp.dot(query, keys, preferred_element_type=jnp.float32) * scale
        scores = jnp.where(live, scores, -1e30)
        top = jnp.max(scores, axis=1, keepdims=True)
        expo = jnp.exp(scores - top)
        total = jnp.sum(expo, axis=1, keepdims=True)
        weights = (expo / total).astype(jnp.bfloat16)
        values = jnp.concatenate([kvt_ref[p, HEADS + h] for p in picks] + [bvt_ref[h]], axis=1)
        ctx = lax.dot_general(
            values, weights, (((1,), (1,)), ((), ())), preferred_element_type=jnp.float32
        )
        o_ref[0, h] = ctx.astype(jnp.bfloat16)


def attention(rel, counts, q, kvt, bkt, bvt):
    nq = q.shape[0]
    nkb = kvt.shape[0]
    head_dim = q.shape[3]
    nbound = bkt.shape[2]
    grid_spec = pltpu.PrefetchScalarGridSpec(
        num_scalar_prefetch=2,
        grid=(nq,),
        in_specs=[
            pl.BlockSpec((1, HEADS, BLOCK, head_dim), lambda b, r, c: (b, 0, 0, 0)),
            pl.BlockSpec((nkb, 2 * HEADS, head_dim, BLOCK), lambda b, r, c: (0, 0, 0, 0)),
            pl.BlockSpec((HEADS, head_dim, nbound), lambda b, r, c: (0, 0, 0)),
            pl.BlockSpec((HEADS, head_dim, nbound), lambda b, r, c: (0, 0, 0)),
        ],
        out_specs=pl.BlockSpec((1, HEADS, head_dim, BLOCK), lambda b, r, c: (b, 0, 0, 0)),
    )
    return pl.pallas_call(
        attention_kernel,
        grid_spec=grid_spec,
        out_shape=jax.ShapeDtypeStruct((nq, HEADS, head_dim, BLOCK), jnp.bfloat16),
    )(rel, counts, q, kvt, bkt, bvt)


def key_tiles(keyvals, width, head_dim):
    rows = keyvals.shape[0]
    keys = keyvals[:, :width].reshape(rows // BLOCK, BLOCK, HEADS, head_dim)
    vals = keyvals[:, width:].reshape(rows // BLOCK, BLOCK, HEADS, head_dim)
    return keys.transpose(0, 2, 3, 1), vals.transpose(0, 2, 3, 1)


def on_device(tokens, w_query, w_keyval, w_out, block_list, block_count, bnd_ids):
    tok_dev, width = tokens.shape
    head_dim = width // HEADS
    nblocks = tok_dev // BLOCK
    member = lax.axis_index("curve")
    queries = jnp.dot(tokens, w_query, preferred_element_type=jnp.float32).astype(jnp.bfloat16)
    queries = queries.reshape(nblocks, BLOCK, HEADS, head_dim).transpose(0, 2, 1, 3)
    pieces = []
    for offset in (-2, -1, 0, 1, 2):
        if offset == 0:
            pieces.append(tokens)
        else:
            pieces.append(from_behind(tokens, "curve", -offset))
    nearby = jnp.concatenate(pieces, axis=0).reshape(5 * nblocks, BLOCK, width)
    kv_w = w_keyval.reshape(width, 2 * HEADS, head_dim).transpose(1, 2, 0)
    kvt = jnp.einsum(
        "hdc,btc->hbdt", kv_w, nearby, preferred_element_type=jnp.float32
    ).astype(jnp.bfloat16)
    kvt = kvt.transpose(1, 0, 2, 3)
    owner = bnd_ids // tok_dev
    local_pos = jnp.clip(bnd_ids - member * tok_dev, 0, tok_dev - 1)
    mine = owner == member
    rows = jnp.where(mine[:, None], jnp.take(tokens, local_pos, axis=0), jnp.zeros((), tokens.dtype))
    gathered = share_rows(rows, owner, member)
    bnd_kv = jnp.dot(gathered, w_keyval, preferred_element_type=jnp.float32).astype(jnp.bfloat16)
    bkt, bvt = key_tiles(bnd_kv, width, head_dim)
    bkt = bkt.transpose(1, 2, 0, 3).reshape(HEADS, head_dim, -1)
    bvt = bvt.transpose(1, 2, 0, 3).reshape(HEADS, head_dim, -1)
    first_block = (member - 2) * nblocks
    rel = jnp.clip(block_list - first_block, 0, 5 * nblocks - 1).reshape(-1).astype(jnp.int32)
    context = attention(rel, block_count.astype(jnp.int32), queries, kvt, bkt, bvt)
    out_w = w_out.reshape(HEADS, head_dim, width)
    mixed = jnp.einsum("bhdt,hde->bte", context, out_w, preferred_element_type=jnp.float32)
    return mixed.reshape(tok_dev, width).astype(jnp.bfloat16)


def solution(mesh):
    in_specs = (
        P(("geo", "curve"), None),
        P(),
        P(),
        P(),
        P(("geo", "curve"), None),
        P(("geo", "curve")),
        P("geo"),
    )
    out_specs = P(("geo", "curve"), None)
    return jax.shard_map(
        on_device, mesh=mesh, in_specs=in_specs, out_specs=out_specs, check_vma=False
    )
```

```python
import jax
import jax.numpy as jnp
from jax import lax
from jax.experimental import pallas as pl
from jax.experimental.pallas import tpu as pltpu
from jax.sharding import PartitionSpec as P

HEADS = 8
BLOCK = 128
NB = 12
BCAP = 128
ROW = 8


def from_behind(value, axis, steps):
    count = lax.axis_size(axis)
    first, last = (max(0, -steps), min(count, count - steps))
    return lax.ppermute(value, axis, [(source, source + steps) for source in range(first, last)])


def share_rows(rows, owner, member, span):
    count = lax.axis_size("curve")
    while span < count:
        pairs = [(source, source ^ span) for source in range(count) if source ^ span < count]
        other = lax.ppermute(rows, "curve", pairs)
        theirs = (owner // span) == ((member // span) ^ 1)
        rows = jnp.where(theirs[:, None], other, rows)
        span *= 2
    return rows


def boundary_rows(tokens, bnd_ids, member):
    tok_dev = tokens.shape[0]
    count = lax.axis_size("curve")
    group = ROW if count % ROW == 0 else 1
    owner = bnd_ids // tok_dev
    my_start = jnp.sum((owner < member).astype(jnp.int32))
    padded_ids = jnp.concatenate([bnd_ids, jnp.zeros((BCAP,), jnp.int32)])
    my_ids = lax.dynamic_slice_in_dim(padded_ids, my_start, BCAP)
    compact = jnp.take(tokens, jnp.clip(my_ids - member * tok_dev, 0, tok_dev - 1), axis=0)
    pieces = [compact]
    for step in range(1, group):
        pairs = [
            (source, (source // group) * group + (source % group + step) % group)
            for source in range(count)
        ]
        pieces.append(lax.ppermute(compact, "curve", pairs))
    near = jnp.concatenate(pieces, axis=0)
    owner_start = jnp.sum((owner[None, :] < owner[:, None]).astype(jnp.int32), axis=1)
    slot = jnp.arange(bnd_ids.shape[0], dtype=jnp.int32)
    within = jnp.clip(slot - owner_start, 0, BCAP - 1)
    step_of = (member % group - owner % group) % group
    rows = jnp.take(near, step_of * BCAP + within, axis=0)
    ours = (owner // group) == (member // group)
    rows = jnp.where(ours[:, None], rows, jnp.zeros((), rows.dtype))
    return share_rows(rows, owner, member, group)


def attention_kernel(rel_ref, cnt_ref, q_ref, kvt_ref, bkt_ref, bvt_ref, o_ref):
    b = pl.program_id(0)
    count = cnt_ref[b]
    picks = [rel_ref[b * NB + i] for i in range(NB)]
    width = NB * BLOCK + bkt_ref.shape[2]
    lane = lax.broadcasted_iota(jnp.int32, (1, width), 1)
    live = (lane // BLOCK < count) | (lane >= NB * BLOCK)
    scale = 1.0 / q_ref.shape[3] ** 0.5
    for h in range(HEADS):
        query = q_ref[0, h]
        keys = jnp.concatenate([kvt_ref[p, h] for p in picks] + [bkt_ref[h]], axis=1)
        scores = jnp.dot(query, keys, preferred_element_type=jnp.float32) * scale
        scores = jnp.where(live, scores, -1e30)
        top = jnp.max(scores, axis=1, keepdims=True)
        expo = jnp.exp(scores - top)
        total = jnp.sum(expo, axis=1, keepdims=True)
        weights = (expo / total).astype(jnp.bfloat16)
        values = jnp.concatenate([kvt_ref[p, HEADS + h] for p in picks] + [bvt_ref[h]], axis=1)
        ctx = lax.dot_general(
            values, weights, (((1,), (1,)), ((), ())), preferred_element_type=jnp.float32
        )
        o_ref[0, h] = ctx.astype(jnp.bfloat16)


def attention(rel, counts, q, kvt, bkt, bvt):
    nq = q.shape[0]
    nkb = kvt.shape[0]
    head_dim = q.shape[3]
    nbound = bkt.shape[2]
    grid_spec = pltpu.PrefetchScalarGridSpec(
        num_scalar_prefetch=2,
        grid=(nq,),
        in_specs=[
            pl.BlockSpec((1, HEADS, BLOCK, head_dim), lambda b, r, c: (b, 0, 0, 0)),
            pl.BlockSpec((nkb, 2 * HEADS, head_dim, BLOCK), lambda b, r, c: (0, 0, 0, 0)),
            pl.BlockSpec((HEADS, head_dim, nbound), lambda b, r, c: (0, 0, 0)),
            pl.BlockSpec((HEADS, head_dim, nbound), lambda b, r, c: (0, 0, 0)),
        ],
        out_specs=pl.BlockSpec((1, HEADS, head_dim, BLOCK), lambda b, r, c: (b, 0, 0, 0)),
    )
    return pl.pallas_call(
        attention_kernel,
        grid_spec=grid_spec,
        out_shape=jax.ShapeDtypeStruct((nq, HEADS, head_dim, BLOCK), jnp.bfloat16),
    )(rel, counts, q, kvt, bkt, bvt)


def key_tiles(keyvals, width, head_dim):
    rows = keyvals.shape[0]
    keys = keyvals[:, :width].reshape(rows // BLOCK, BLOCK, HEADS, head_dim)
    vals = keyvals[:, width:].reshape(rows // BLOCK, BLOCK, HEADS, head_dim)
    return keys.transpose(0, 2, 3, 1), vals.transpose(0, 2, 3, 1)


def on_device(tokens, w_query, w_keyval, w_out, block_list, block_count, bnd_ids):
    tok_dev, width = tokens.shape
    head_dim = width // HEADS
    nblocks = tok_dev // BLOCK
    member = lax.axis_index("curve")
    queries = jnp.dot(tokens, w_query, preferred_element_type=jnp.float32).astype(jnp.bfloat16)
    queries = queries.reshape(nblocks, BLOCK, HEADS, head_dim).transpose(0, 2, 1, 3)
    pieces = []
    for offset in (-2, -1, 0, 1, 2):
        if offset == 0:
            pieces.append(tokens)
        else:
            pieces.append(from_behind(tokens, "curve", -offset))
    nearby = jnp.concatenate(pieces, axis=0).reshape(5 * nblocks, BLOCK, width)
    kv_w = w_keyval.reshape(width, 2 * HEADS, head_dim).transpose(1, 2, 0)
    kvt = jnp.einsum(
        "hdc,btc->hbdt", kv_w, nearby, preferred_element_type=jnp.float32
    ).astype(jnp.bfloat16)
    kvt = kvt.transpose(1, 0, 2, 3)
    gathered = boundary_rows(tokens, bnd_ids, member)
    bnd_kv = jnp.dot(gathered, w_keyval, preferred_element_type=jnp.float32).astype(jnp.bfloat16)
    bkt, bvt = key_tiles(bnd_kv, width, head_dim)
    bkt = bkt.transpose(1, 2, 0, 3).reshape(HEADS, head_dim, -1)
    bvt = bvt.transpose(1, 2, 0, 3).reshape(HEADS, head_dim, -1)
    first_block = (member - 2) * nblocks
    rel = jnp.clip(block_list - first_block, 0, 5 * nblocks - 1).reshape(-1).astype(jnp.int32)
    context = attention(rel, block_count.astype(jnp.int32), queries, kvt, bkt, bvt)
    out_w = w_out.reshape(HEADS, head_dim, width)
    mixed = jnp.einsum("bhdt,hde->bte", context, out_w, preferred_element_type=jnp.float32)
    return mixed.reshape(tok_dev, width).astype(jnp.bfloat16)


def solution(mesh):
    in_specs = (
        P(("geo", "curve"), None),
        P(),
        P(),
        P(),
        P(("geo", "curve"), None),
        P(("geo", "curve")),
        P("geo"),
    )
    out_specs = P(("geo", "curve"), None)
    return jax.shard_map(
        on_device, mesh=mesh, in_specs=in_specs, out_specs=out_specs, check_vma=False
    )
```

```python
import jax
import jax.numpy as jnp
from jax import lax
from jax.experimental import pallas as pl
from jax.experimental.pallas import tpu as pltpu
from jax.sharding import PartitionSpec as P

HEADS = 8
BLOCK = 128
NB = 12
BCAP = 128
ROW = 8


def from_behind(value, axis, steps):
    count = lax.axis_size(axis)
    first, last = (max(0, -steps), min(count, count - steps))
    return lax.ppermute(value, axis, [(source, source + steps) for source in range(first, last)])


def share_rows(rows, owner, member, span):
    count = lax.axis_size("curve")
    while span < count:
        pairs = [(source, source ^ span) for source in range(count) if source ^ span < count]
        other = lax.ppermute(rows, "curve", pairs)
        theirs = (owner // span) == ((member // span) ^ 1)
        rows = jnp.where(theirs[:, None], other, rows)
        span *= 2
    return rows


def boundary_rows(tokens, bnd_ids, member):
    tok_dev = tokens.shape[0]
    count = lax.axis_size("curve")
    group = ROW if count % ROW == 0 else 1
    owner = bnd_ids // tok_dev
    my_start = jnp.sum((owner < member).astype(jnp.int32))
    padded_ids = jnp.concatenate([bnd_ids, jnp.zeros((BCAP,), jnp.int32)])
    my_ids = lax.dynamic_slice_in_dim(padded_ids, my_start, BCAP)
    compact = jnp.take(tokens, jnp.clip(my_ids - member * tok_dev, 0, tok_dev - 1), axis=0)
    pieces = [compact]
    for step in range(1, group):
        pairs = [
            (source, (source // group) * group + (source % group + step) % group)
            for source in range(count)
        ]
        pieces.append(lax.ppermute(compact, "curve", pairs))
    near = jnp.concatenate(pieces, axis=0)
    owner_start = jnp.sum((owner[None, :] < owner[:, None]).astype(jnp.int32), axis=1)
    slot = jnp.arange(bnd_ids.shape[0], dtype=jnp.int32)
    within = jnp.clip(slot - owner_start, 0, BCAP - 1)
    step_of = (member % group - owner % group) % group
    rows = jnp.take(near, step_of * BCAP + within, axis=0)
    ours = (owner // group) == (member // group)
    rows = jnp.where(ours[:, None], rows, jnp.zeros((), rows.dtype))
    return share_rows(rows, owner, member, group)


def attention_kernel(rel_ref, cnt_ref, q_ref, kvt_ref, bkt_ref, bvt_ref, o_ref):
    b = pl.program_id(0)
    count = cnt_ref[b]
    picks = [rel_ref[b * NB + i] for i in range(NB)]
    width = NB * BLOCK + bkt_ref.shape[2]
    lane = lax.broadcasted_iota(jnp.int32, (1, width), 1)
    live = (lane // BLOCK < count) | (lane >= NB * BLOCK)
    scale = 1.0 / q_ref.shape[3] ** 0.5
    for h in range(HEADS):
        query = q_ref[0, h]
        keys = jnp.concatenate([kvt_ref[p, h] for p in picks] + [bkt_ref[h]], axis=1)
        scores = jnp.dot(query, keys, preferred_element_type=jnp.float32) * scale
        scores = jnp.where(live, scores, -1e30)
        top = jnp.max(scores, axis=1, keepdims=True)
        expo = jnp.exp(scores - top)
        total = jnp.sum(expo, axis=1, keepdims=True)
        weights = (expo * (1.0 / total)).astype(jnp.bfloat16)
        values = jnp.concatenate([kvt_ref[p, HEADS + h] for p in picks] + [bvt_ref[h]], axis=1)
        ctx = lax.dot_general(
            values, weights, (((1,), (1,)), ((), ())), preferred_element_type=jnp.float32
        )
        o_ref[0, h] = ctx.astype(jnp.bfloat16)


def attention(rel, counts, q, kvt, bkt, bvt):
    nq = q.shape[0]
    nkb = kvt.shape[0]
    head_dim = q.shape[3]
    nbound = bkt.shape[2]
    grid_spec = pltpu.PrefetchScalarGridSpec(
        num_scalar_prefetch=2,
        grid=(nq,),
        in_specs=[
            pl.BlockSpec((1, HEADS, BLOCK, head_dim), lambda b, r, c: (b, 0, 0, 0)),
            pl.BlockSpec((nkb, 2 * HEADS, head_dim, BLOCK), lambda b, r, c: (0, 0, 0, 0)),
            pl.BlockSpec((HEADS, head_dim, nbound), lambda b, r, c: (0, 0, 0)),
            pl.BlockSpec((HEADS, head_dim, nbound), lambda b, r, c: (0, 0, 0)),
        ],
        out_specs=pl.BlockSpec((1, HEADS, head_dim, BLOCK), lambda b, r, c: (b, 0, 0, 0)),
    )
    return pl.pallas_call(
        attention_kernel,
        grid_spec=grid_spec,
        out_shape=jax.ShapeDtypeStruct((nq, HEADS, head_dim, BLOCK), jnp.bfloat16),
    )(rel, counts, q, kvt, bkt, bvt)


def key_tiles(keyvals, width, head_dim):
    rows = keyvals.shape[0]
    keys = keyvals[:, :width].reshape(rows // BLOCK, BLOCK, HEADS, head_dim)
    vals = keyvals[:, width:].reshape(rows // BLOCK, BLOCK, HEADS, head_dim)
    return keys.transpose(0, 2, 3, 1), vals.transpose(0, 2, 3, 1)


def on_device(tokens, w_query, w_keyval, w_out, block_list, block_count, bnd_ids):
    tok_dev, width = tokens.shape
    head_dim = width // HEADS
    nblocks = tok_dev // BLOCK
    member = lax.axis_index("curve")
    queries = jnp.dot(tokens, w_query, preferred_element_type=jnp.float32).astype(jnp.bfloat16)
    queries = queries.reshape(nblocks, BLOCK, HEADS, head_dim).transpose(0, 2, 1, 3)
    pieces = []
    for offset in (-2, -1, 0, 1, 2):
        if offset == 0:
            pieces.append(tokens)
        else:
            pieces.append(from_behind(tokens, "curve", -offset))
    kv_w = w_keyval.reshape(width, 2 * HEADS, head_dim).transpose(1, 2, 0)
    kvt = jnp.zeros((5 * nblocks, 2 * HEADS, head_dim, BLOCK), jnp.bfloat16)
    for index in (2, 0, 1, 3, 4):
        piece = pieces[index]
        part = jnp.einsum(
            "hdc,btc->bhdt",
            kv_w,
            piece.reshape(nblocks, BLOCK, width),
            preferred_element_type=jnp.float32,
        ).astype(jnp.bfloat16)
        kvt = kvt.at[index * nblocks : (index + 1) * nblocks].set(part)
    gathered = boundary_rows(tokens, bnd_ids, member)
    bnd_kv = jnp.dot(gathered, w_keyval, preferred_element_type=jnp.float32).astype(jnp.bfloat16)
    bkt, bvt = key_tiles(bnd_kv, width, head_dim)
    bkt = bkt.transpose(1, 2, 0, 3).reshape(HEADS, head_dim, -1)
    bvt = bvt.transpose(1, 2, 0, 3).reshape(HEADS, head_dim, -1)
    first_block = (member - 2) * nblocks
    rel = jnp.clip(block_list - first_block, 0, 5 * nblocks - 1).reshape(-1).astype(jnp.int32)
    context = attention(rel, block_count.astype(jnp.int32), queries, kvt, bkt, bvt)
    out_w = w_out.reshape(HEADS, head_dim, width)
    mixed = jnp.einsum("bhdt,hde->bte", context, out_w, preferred_element_type=jnp.float32)
    return mixed.reshape(tok_dev, width).astype(jnp.bfloat16)


def solution(mesh):
    in_specs = (
        P(("geo", "curve"), None),
        P(),
        P(),
        P(),
        P(("geo", "curve"), None),
        P(("geo", "curve")),
        P("geo"),
    )
    out_specs = P(("geo", "curve"), None)
    return jax.shard_map(
        on_device, mesh=mesh, in_specs=in_specs, out_specs=out_specs, check_vma=False
    )
```

```python
import jax
import jax.numpy as jnp
from jax import lax
from jax.experimental import pallas as pl
from jax.experimental.pallas import tpu as pltpu
from jax.sharding import PartitionSpec as P

HEADS = 8
BLOCK = 128
NB = 12
BCAP = 128
ROW = 8
CLASSES = (4, 8, NB)
LOG2E = 1.4426950408889634


def from_behind(value, axis, steps):
    count = lax.axis_size(axis)
    first, last = (max(0, -steps), min(count, count - steps))
    return lax.ppermute(value, axis, [(source, source + steps) for source in range(first, last)])


def share_rows(rows, owner, member, span):
    count = lax.axis_size("curve")
    while span < count:
        pairs = [(source, source ^ span) for source in range(count) if source ^ span < count]
        other = lax.ppermute(rows, "curve", pairs)
        theirs = (owner // span) == ((member // span) ^ 1)
        rows = jnp.where(theirs[:, None], other, rows)
        span *= 2
    return rows


def boundary_rows(tokens, bnd_ids, member):
    tok_dev = tokens.shape[0]
    count = lax.axis_size("curve")
    group = ROW if count % ROW == 0 else 1
    owner = bnd_ids // tok_dev
    my_start = jnp.sum((owner < member).astype(jnp.int32))
    padded_ids = jnp.concatenate([bnd_ids, jnp.zeros((BCAP,), jnp.int32)])
    my_ids = lax.dynamic_slice_in_dim(padded_ids, my_start, BCAP)
    compact = jnp.take(tokens, jnp.clip(my_ids - member * tok_dev, 0, tok_dev - 1), axis=0)
    pieces = [compact]
    for step in range(1, group):
        pairs = [
            (source, (source // group) * group + (source % group + step) % group)
            for source in range(count)
        ]
        pieces.append(lax.ppermute(compact, "curve", pairs))
    near = jnp.concatenate(pieces, axis=0)
    owner_start = jnp.sum((owner[None, :] < owner[:, None]).astype(jnp.int32), axis=1)
    slot = jnp.arange(bnd_ids.shape[0], dtype=jnp.int32)
    within = jnp.clip(slot - owner_start, 0, BCAP - 1)
    step_of = (member % group - owner % group) % group
    rows = jnp.take(near, step_of * BCAP + within, axis=0)
    ours = (owner // group) == (member // group)
    rows = jnp.where(ours[:, None], rows, jnp.zeros((), rows.dtype))
    return share_rows(rows, owner, member, group)


def attend_heads(picks, count, q_ref, kvt_ref, bkt_ref, bvt_ref, o_ref):
    near = len(picks) * BLOCK
    width = near + bkt_ref.shape[2]
    lane = lax.broadcasted_iota(jnp.int32, (1, width), 1)
    live = (lane // BLOCK < count) | (lane >= near)
    rate = LOG2E / q_ref.shape[3] ** 0.5
    for h in range(HEADS):
        query = q_ref[0, h]
        keys = jnp.concatenate([kvt_ref[p, h] for p in picks] + [bkt_ref[h]], axis=1)
        scores = jnp.dot(query, keys, preferred_element_type=jnp.float32)
        scores = jnp.where(live, scores, -1e30)
        top = jnp.max(scores, axis=1, keepdims=True)
        expo = jnp.exp2((scores - top) * rate)
        total = jnp.sum(expo, axis=1, keepdims=True)
        weights = (expo * (1.0 / total)).astype(jnp.bfloat16)
        values = jnp.concatenate([kvt_ref[p, HEADS + h] for p in picks] + [bvt_ref[h]], axis=1)
        ctx = lax.dot_general(
            values, weights, (((1,), (1,)), ((), ())), preferred_element_type=jnp.float32
        )
        o_ref[0, h] = ctx.astype(jnp.bfloat16)


def attention_kernel(rel_ref, cnt_ref, q_ref, kvt_ref, bkt_ref, bvt_ref, o_ref):
    b = pl.program_id(0)
    count = cnt_ref[b]
    picks = [rel_ref[b * NB + i] for i in range(NB)]
    low = 0
    for high in CLASSES:

        @pl.when((count > low) & (count <= high))
        def _():
            attend_heads(picks[:high], count, q_ref, kvt_ref, bkt_ref, bvt_ref, o_ref)

        low = high


def attention(rel, counts, q, kvt, bkt, bvt):
    nq = q.shape[0]
    nkb = kvt.shape[0]
    head_dim = q.shape[3]
    nbound = bkt.shape[2]
    grid_spec = pltpu.PrefetchScalarGridSpec(
        num_scalar_prefetch=2,
        grid=(nq,),
        in_specs=[
            pl.BlockSpec((1, HEADS, BLOCK, head_dim), lambda b, r, c: (b, 0, 0, 0)),
            pl.BlockSpec((nkb, 2 * HEADS, head_dim, BLOCK), lambda b, r, c: (0, 0, 0, 0)),
            pl.BlockSpec((HEADS, head_dim, nbound), lambda b, r, c: (0, 0, 0)),
            pl.BlockSpec((HEADS, head_dim, nbound), lambda b, r, c: (0, 0, 0)),
        ],
        out_specs=pl.BlockSpec((1, HEADS, head_dim, BLOCK), lambda b, r, c: (b, 0, 0, 0)),
    )
    return pl.pallas_call(
        attention_kernel,
        grid_spec=grid_spec,
        out_shape=jax.ShapeDtypeStruct((nq, HEADS, head_dim, BLOCK), jnp.bfloat16),
    )(rel, counts, q, kvt, bkt, bvt)


def key_tiles(keyvals, width, head_dim):
    rows = keyvals.shape[0]
    keys = keyvals[:, :width].reshape(rows // BLOCK, BLOCK, HEADS, head_dim)
    vals = keyvals[:, width:].reshape(rows // BLOCK, BLOCK, HEADS, head_dim)
    return keys.transpose(0, 2, 3, 1), vals.transpose(0, 2, 3, 1)


def on_device(tokens, w_query, w_keyval, w_out, block_list, block_count, bnd_ids):
    tok_dev, width = tokens.shape
    head_dim = width // HEADS
    nblocks = tok_dev // BLOCK
    member = lax.axis_index("curve")
    queries = jnp.dot(tokens, w_query, preferred_element_type=jnp.float32).astype(jnp.bfloat16)
    queries = queries.reshape(nblocks, BLOCK, HEADS, head_dim).transpose(0, 2, 1, 3)
    pieces = []
    for offset in (-2, -1, 0, 1, 2):
        if offset == 0:
            pieces.append(tokens)
        else:
            pieces.append(from_behind(tokens, "curve", -offset))
    kv_w = w_keyval.reshape(width, 2 * HEADS, head_dim).transpose(1, 2, 0)
    kvt = jnp.zeros((5 * nblocks, 2 * HEADS, head_dim, BLOCK), jnp.bfloat16)
    for index in (2, 0, 1, 3, 4):
        piece = pieces[index]
        part = jnp.einsum(
            "hdc,btc->bhdt",
            kv_w,
            piece.reshape(nblocks, BLOCK, width),
            preferred_element_type=jnp.float32,
        ).astype(jnp.bfloat16)
        kvt = kvt.at[index * nblocks : (index + 1) * nblocks].set(part)
    gathered = boundary_rows(tokens, bnd_ids, member)
    bnd_kv = jnp.dot(gathered, w_keyval, preferred_element_type=jnp.float32).astype(jnp.bfloat16)
    bkt, bvt = key_tiles(bnd_kv, width, head_dim)
    bkt = bkt.transpose(1, 2, 0, 3).reshape(HEADS, head_dim, -1)
    bvt = bvt.transpose(1, 2, 0, 3).reshape(HEADS, head_dim, -1)
    first_block = (member - 2) * nblocks
    rel = jnp.clip(block_list - first_block, 0, 5 * nblocks - 1).reshape(-1).astype(jnp.int32)
    context = attention(rel, block_count.astype(jnp.int32), queries, kvt, bkt, bvt)
    out_w = w_out.reshape(HEADS, head_dim, width)
    mixed = jnp.einsum("bhdt,hde->bte", context, out_w, preferred_element_type=jnp.float32)
    return mixed.reshape(tok_dev, width).astype(jnp.bfloat16)


def solution(mesh):
    in_specs = (
        P(("geo", "curve"), None),
        P(),
        P(),
        P(),
        P(("geo", "curve"), None),
        P(("geo", "curve")),
        P("geo"),
    )
    out_specs = P(("geo", "curve"), None)
    return jax.shard_map(
        on_device, mesh=mesh, in_specs=in_specs, out_specs=out_specs, check_vma=False
    )
```

```python
import jax
import jax.numpy as jnp
from jax import lax
from jax.experimental import pallas as pl
from jax.experimental.pallas import tpu as pltpu
from jax.sharding import PartitionSpec as P

HEADS = 8
BLOCK = 128
NB = 12
BCAP = 128
ROW = 8
CLASSES = (4, 8, NB)
LOG2E = 1.4426950408889634


def from_behind(value, axis, steps):
    count = lax.axis_size(axis)
    first, last = (max(0, -steps), min(count, count - steps))
    return lax.ppermute(value, axis, [(source, source + steps) for source in range(first, last)])


def share_rows(rows, owner, member, span):
    count = lax.axis_size("curve")
    while span < count:
        pairs = [(source, source ^ span) for source in range(count) if source ^ span < count]
        other = lax.ppermute(rows, "curve", pairs)
        theirs = (owner // span) == ((member // span) ^ 1)
        rows = jnp.where(theirs[:, None], other, rows)
        span *= 2
    return rows


def boundary_rows(tokens, bnd_ids, member):
    tok_dev = tokens.shape[0]
    count = lax.axis_size("curve")
    group = ROW if count % ROW == 0 else 1
    owner = bnd_ids // tok_dev
    my_start = jnp.sum((owner < member).astype(jnp.int32))
    padded_ids = jnp.concatenate([bnd_ids, jnp.zeros((BCAP,), jnp.int32)])
    my_ids = lax.dynamic_slice_in_dim(padded_ids, my_start, BCAP)
    compact = jnp.take(tokens, jnp.clip(my_ids - member * tok_dev, 0, tok_dev - 1), axis=0)
    pieces = [compact]
    for step in range(1, group):
        pairs = [
            (source, (source // group) * group + (source % group + step) % group)
            for source in range(count)
        ]
        pieces.append(lax.ppermute(compact, "curve", pairs))
    near = jnp.concatenate(pieces, axis=0)
    owner_start = jnp.sum((owner[None, :] < owner[:, None]).astype(jnp.int32), axis=1)
    slot = jnp.arange(bnd_ids.shape[0], dtype=jnp.int32)
    within = jnp.clip(slot - owner_start, 0, BCAP - 1)
    step_of = (member % group - owner % group) % group
    rows = jnp.take(near, step_of * BCAP + within, axis=0)
    ours = (owner // group) == (member // group)
    rows = jnp.where(ours[:, None], rows, jnp.zeros((), rows.dtype))
    return share_rows(rows, owner, member, group)


def attend_heads(picks, count, q_ref, kvt_ref, bkt_ref, bvt_ref, w_ref, o_ref):
    near = len(picks) * BLOCK
    width = near + bkt_ref.shape[2]
    lane = lax.broadcasted_iota(jnp.int32, (1, width), 1)
    live = (lane // BLOCK < count) | (lane >= near)
    rate = LOG2E / q_ref.shape[3] ** 0.5
    contexts = []
    for h in range(HEADS):
        query = q_ref[0, h]
        keys = jnp.concatenate([kvt_ref[p, h] for p in picks] + [bkt_ref[h]], axis=1)
        scores = jnp.dot(query, keys, preferred_element_type=jnp.float32)
        scores = jnp.where(live, scores, -1e30)
        top = jnp.max(scores, axis=1, keepdims=True)
        expo = jnp.exp2((scores - top) * rate)
        total = jnp.sum(expo, axis=1, keepdims=True)
        weights = (expo * (1.0 / total)).astype(jnp.bfloat16)
        values = jnp.concatenate([kvt_ref[p, HEADS + h] for p in picks] + [bvt_ref[h]], axis=1)
        ctx = lax.dot_general(
            values, weights, (((1,), (1,)), ((), ())), preferred_element_type=jnp.float32
        )
        contexts.append(ctx.astype(jnp.bfloat16))
    context = jnp.concatenate(contexts, axis=0)
    mixed = lax.dot_general(
        context, w_ref[...], (((0,), (0,)), ((), ())), preferred_element_type=jnp.float32
    )
    o_ref[0] = mixed.astype(jnp.bfloat16)


def attention_kernel(rel_ref, cnt_ref, q_ref, kvt_ref, bkt_ref, bvt_ref, w_ref, o_ref):
    b = pl.program_id(0)
    count = cnt_ref[b]
    picks = [rel_ref[b * NB + i] for i in range(NB)]
    low = 0
    for high in CLASSES:

        @pl.when((count > low) & (count <= high))
        def _():
            attend_heads(picks[:high], count, q_ref, kvt_ref, bkt_ref, bvt_ref, w_ref, o_ref)

        low = high


def attention(rel, counts, q, kvt, bkt, bvt, w_out):
    nq = q.shape[0]
    nkb = kvt.shape[0]
    head_dim = q.shape[3]
    nbound = bkt.shape[2]
    width = w_out.shape[0]
    grid_spec = pltpu.PrefetchScalarGridSpec(
        num_scalar_prefetch=2,
        grid=(nq,),
        in_specs=[
            pl.BlockSpec((1, HEADS, BLOCK, head_dim), lambda b, r, c: (b, 0, 0, 0)),
            pl.BlockSpec((nkb, 2 * HEADS, head_dim, BLOCK), lambda b, r, c: (0, 0, 0, 0)),
            pl.BlockSpec((HEADS, head_dim, nbound), lambda b, r, c: (0, 0, 0)),
            pl.BlockSpec((HEADS, head_dim, nbound), lambda b, r, c: (0, 0, 0)),
            pl.BlockSpec((width, width), lambda b, r, c: (0, 0)),
        ],
        out_specs=pl.BlockSpec((1, BLOCK, width), lambda b, r, c: (b, 0, 0)),
    )
    return pl.pallas_call(
        attention_kernel,
        grid_spec=grid_spec,
        out_shape=jax.ShapeDtypeStruct((nq, BLOCK, width), jnp.bfloat16),
    )(rel, counts, q, kvt, bkt, bvt, w_out)


def key_tiles(keyvals, width, head_dim):
    rows = keyvals.shape[0]
    keys = keyvals[:, :width].reshape(rows // BLOCK, BLOCK, HEADS, head_dim)
    vals = keyvals[:, width:].reshape(rows // BLOCK, BLOCK, HEADS, head_dim)
    return keys.transpose(0, 2, 3, 1), vals.transpose(0, 2, 3, 1)


def on_device(tokens, w_query, w_keyval, w_out, block_list, block_count, bnd_ids):
    tok_dev, width = tokens.shape
    head_dim = width // HEADS
    nblocks = tok_dev // BLOCK
    member = lax.axis_index("curve")
    queries = jnp.dot(tokens, w_query, preferred_element_type=jnp.float32).astype(jnp.bfloat16)
    queries = queries.reshape(nblocks, BLOCK, HEADS, head_dim).transpose(0, 2, 1, 3)
    pieces = []
    for offset in (-2, -1, 0, 1, 2):
        if offset == 0:
            pieces.append(tokens)
        else:
            pieces.append(from_behind(tokens, "curve", -offset))
    kv_w = w_keyval.reshape(width, 2 * HEADS, head_dim).transpose(1, 2, 0)
    kvt = jnp.zeros((5 * nblocks, 2 * HEADS, head_dim, BLOCK), jnp.bfloat16)
    for index in (2, 0, 1, 3, 4):
        piece = pieces[index]
        part = jnp.einsum(
            "hdc,btc->bhdt",
            kv_w,
            piece.reshape(nblocks, BLOCK, width),
            preferred_element_type=jnp.float32,
        ).astype(jnp.bfloat16)
        kvt = kvt.at[index * nblocks : (index + 1) * nblocks].set(part)
    gathered = boundary_rows(tokens, bnd_ids, member)
    bnd_kv = jnp.dot(gathered, w_keyval, preferred_element_type=jnp.float32).astype(jnp.bfloat16)
    bkt, bvt = key_tiles(bnd_kv, width, head_dim)
    bkt = bkt.transpose(1, 2, 0, 3).reshape(HEADS, head_dim, -1)
    bvt = bvt.transpose(1, 2, 0, 3).reshape(HEADS, head_dim, -1)
    first_block = (member - 2) * nblocks
    rel = jnp.clip(block_list - first_block, 0, 5 * nblocks - 1).reshape(-1).astype(jnp.int32)
    mixed = attention(rel, block_count.astype(jnp.int32), queries, kvt, bkt, bvt, w_out)
    return mixed.reshape(tok_dev, width)


def solution(mesh):
    in_specs = (
        P(("geo", "curve"), None),
        P(),
        P(),
        P(),
        P(("geo", "curve"), None),
        P(("geo", "curve")),
        P("geo"),
    )
    out_specs = P(("geo", "curve"), None)
    return jax.shard_map(
        on_device, mesh=mesh, in_specs=in_specs, out_specs=out_specs, check_vma=False
    )
```

```python
import jax
import jax.numpy as jnp
from jax import lax
from jax.experimental import pallas as pl
from jax.experimental.pallas import tpu as pltpu
from jax.sharding import PartitionSpec as P

HEADS = 8
BLOCK = 128
NB = 12
BCAP = 128
ROW = 8
CURVE = ("cy", "cz")
CLASSES = (4, 8, NB)
LOG2E = 1.4426950408889634


def from_behind(value, axis, steps):
    count = lax.axis_size(axis)
    first, last = (max(0, -steps), min(count, count - steps))
    return lax.ppermute(value, axis, [(source, source + steps) for source in range(first, last)])


def share_rows(rows, owner, member, span):
    count = lax.axis_size(CURVE)
    while span < count:
        pairs = [(source, source ^ span) for source in range(count) if source ^ span < count]
        other = lax.ppermute(rows, CURVE, pairs)
        theirs = (owner // span) == ((member // span) ^ 1)
        rows = jnp.where(theirs[:, None], other, rows)
        span *= 2
    return rows


def boundary_rows(tokens, bnd_ids, member):
    tok_dev = tokens.shape[0]
    group = lax.axis_size("cz")
    owner = bnd_ids // tok_dev
    my_start = jnp.sum((owner < member).astype(jnp.int32))
    padded_ids = jnp.concatenate([bnd_ids, jnp.zeros((BCAP,), jnp.int32)])
    my_ids = lax.dynamic_slice_in_dim(padded_ids, my_start, BCAP)
    compact = jnp.take(tokens, jnp.clip(my_ids - member * tok_dev, 0, tok_dev - 1), axis=0)
    near = lax.all_gather(compact, "cz", axis=0, tiled=True)
    owner_start = jnp.sum((owner[None, :] < owner[:, None]).astype(jnp.int32), axis=1)
    slot = jnp.arange(bnd_ids.shape[0], dtype=jnp.int32)
    within = jnp.clip(slot - owner_start, 0, BCAP - 1)
    rows = jnp.take(near, (owner % group) * BCAP + within, axis=0)
    ours = (owner // group) == (member // group)
    rows = jnp.where(ours[:, None], rows, jnp.zeros((), rows.dtype))
    return share_rows(rows, owner, member, group)


def attend_heads(picks, count, q_ref, kvt_ref, bkt_ref, bvt_ref, w_ref, o_ref):
    near = len(picks) * BLOCK
    width = near + bkt_ref.shape[2]
    lane = lax.broadcasted_iota(jnp.int32, (1, width), 1)
    live = (lane // BLOCK < count) | (lane >= near)
    rate = LOG2E / q_ref.shape[3] ** 0.5
    contexts = []
    for h in range(HEADS):
        query = q_ref[0, h]
        keys = jnp.concatenate([kvt_ref[p, h] for p in picks] + [bkt_ref[h]], axis=1)
        scores = jnp.dot(query, keys, preferred_element_type=jnp.float32)
        scores = jnp.where(live, scores, -1e30)
        top = jnp.max(scores, axis=1, keepdims=True)
        expo = jnp.exp2((scores - top) * rate)
        total = jnp.sum(expo, axis=1, keepdims=True)
        weights = (expo * (1.0 / total)).astype(jnp.bfloat16)
        values = jnp.concatenate([kvt_ref[p, HEADS + h] for p in picks] + [bvt_ref[h]], axis=1)
        ctx = lax.dot_general(
            values, weights, (((1,), (1,)), ((), ())), preferred_element_type=jnp.float32
        )
        contexts.append(ctx.astype(jnp.bfloat16))
    context = jnp.concatenate(contexts, axis=0)
    mixed = lax.dot_general(
        context, w_ref[...], (((0,), (0,)), ((), ())), preferred_element_type=jnp.float32
    )
    o_ref[0] = mixed.astype(jnp.bfloat16)


def attention_kernel(rel_ref, cnt_ref, q_ref, kvt_ref, bkt_ref, bvt_ref, w_ref, o_ref):
    b = pl.program_id(0)
    count = cnt_ref[b]
    picks = [rel_ref[b * NB + i] for i in range(NB)]
    low = 0
    for high in CLASSES:

        @pl.when((count > low) & (count <= high))
        def _():
            attend_heads(picks[:high], count, q_ref, kvt_ref, bkt_ref, bvt_ref, w_ref, o_ref)

        low = high


def attention(rel, counts, q, kvt, bkt, bvt, w_out):
    nq = q.shape[0]
    nkb = kvt.shape[0]
    head_dim = q.shape[3]
    nbound = bkt.shape[2]
    width = w_out.shape[0]
    grid_spec = pltpu.PrefetchScalarGridSpec(
        num_scalar_prefetch=2,
        grid=(nq,),
        in_specs=[
            pl.BlockSpec((1, HEADS, BLOCK, head_dim), lambda b, r, c: (b, 0, 0, 0)),
            pl.BlockSpec((nkb, 2 * HEADS, head_dim, BLOCK), lambda b, r, c: (0, 0, 0, 0)),
            pl.BlockSpec((HEADS, head_dim, nbound), lambda b, r, c: (0, 0, 0)),
            pl.BlockSpec((HEADS, head_dim, nbound), lambda b, r, c: (0, 0, 0)),
            pl.BlockSpec((width, width), lambda b, r, c: (0, 0)),
        ],
        out_specs=pl.BlockSpec((1, BLOCK, width), lambda b, r, c: (b, 0, 0)),
    )
    return pl.pallas_call(
        attention_kernel,
        grid_spec=grid_spec,
        out_shape=jax.ShapeDtypeStruct((nq, BLOCK, width), jnp.bfloat16),
    )(rel, counts, q, kvt, bkt, bvt, w_out)


def key_tiles(keyvals, width, head_dim):
    rows = keyvals.shape[0]
    keys = keyvals[:, :width].reshape(rows // BLOCK, BLOCK, HEADS, head_dim)
    vals = keyvals[:, width:].reshape(rows // BLOCK, BLOCK, HEADS, head_dim)
    return keys.transpose(0, 2, 3, 1), vals.transpose(0, 2, 3, 1)


def on_device(tokens, w_query, w_keyval, w_out, block_list, block_count, bnd_ids):
    tok_dev, width = tokens.shape
    head_dim = width // HEADS
    nblocks = tok_dev // BLOCK
    member = lax.axis_index(CURVE)
    queries = jnp.dot(tokens, w_query, preferred_element_type=jnp.float32).astype(jnp.bfloat16)
    queries = queries.reshape(nblocks, BLOCK, HEADS, head_dim).transpose(0, 2, 1, 3)
    pieces = []
    for offset in (-2, -1, 0, 1, 2):
        if offset == 0:
            pieces.append(tokens)
        else:
            pieces.append(from_behind(tokens, CURVE, -offset))
    kv_w = w_keyval.reshape(width, 2 * HEADS, head_dim).transpose(1, 2, 0)
    kvt = jnp.zeros((5 * nblocks, 2 * HEADS, head_dim, BLOCK), jnp.bfloat16)
    for index in (2, 0, 1, 3, 4):
        piece = pieces[index]
        part = jnp.einsum(
            "hdc,btc->bhdt",
            kv_w,
            piece.reshape(nblocks, BLOCK, width),
            preferred_element_type=jnp.float32,
        ).astype(jnp.bfloat16)
        kvt = kvt.at[index * nblocks : (index + 1) * nblocks].set(part)
    gathered = boundary_rows(tokens, bnd_ids, member)
    bnd_kv = jnp.dot(gathered, w_keyval, preferred_element_type=jnp.float32).astype(jnp.bfloat16)
    bkt, bvt = key_tiles(bnd_kv, width, head_dim)
    bkt = bkt.transpose(1, 2, 0, 3).reshape(HEADS, head_dim, -1)
    bvt = bvt.transpose(1, 2, 0, 3).reshape(HEADS, head_dim, -1)
    first_block = (member - 2) * nblocks
    rel = jnp.clip(block_list - first_block, 0, 5 * nblocks - 1).reshape(-1).astype(jnp.int32)
    mixed = attention(rel, block_count.astype(jnp.int32), queries, kvt, bkt, bvt, w_out)
    return mixed.reshape(tok_dev, width)


def solution(mesh):
    curve = mesh.shape["curve"]
    row = ROW if curve % ROW == 0 else 1
    devices = mesh.devices.reshape(mesh.shape["geo"], curve // row, row)
    split = jax.sharding.Mesh(devices, ("geo",) + CURVE)
    rows = P(("geo",) + CURVE, None)
    in_specs = (rows, P(), P(), P(), rows, P(("geo",) + CURVE), P("geo"))
    return jax.shard_map(on_device, mesh=split, in_specs=in_specs, out_specs=rows, check_vma=False)
```

```python
import jax
import jax.numpy as jnp
from jax import lax
from jax.experimental import pallas as pl
from jax.experimental.pallas import tpu as pltpu
from jax.sharding import PartitionSpec as P

HEADS = 8
BLOCK = 128
NB = 12
BCAP = 128
ROW = 8
CLASSES = (4, 8, NB)
LOG2E = 1.4426950408889634


def from_behind(value, axis, steps):
    count = lax.axis_size(axis)
    first, last = (max(0, -steps), min(count, count - steps))
    return lax.ppermute(value, axis, [(source, source + steps) for source in range(first, last)])


def share_rows(rows, owner, member, span):
    count = lax.axis_size("curve")
    while span < count:
        pairs = [(source, source ^ span) for source in range(count) if source ^ span < count]
        other = lax.ppermute(rows, "curve", pairs)
        theirs = (owner // span) == ((member // span) ^ 1)
        rows = jnp.where(theirs[:, None], other, rows)
        span *= 2
    return rows


def boundary_rows(tokens, bnd_ids, member):
    tok_dev = tokens.shape[0]
    count = lax.axis_size("curve")
    group = ROW if count % ROW == 0 else 1
    owner = bnd_ids // tok_dev
    my_start = jnp.sum((owner < member).astype(jnp.int32))
    padded_ids = jnp.concatenate([bnd_ids, jnp.zeros((BCAP,), jnp.int32)])
    my_ids = lax.dynamic_slice_in_dim(padded_ids, my_start, BCAP)
    compact = jnp.take(tokens, jnp.clip(my_ids - member * tok_dev, 0, tok_dev - 1), axis=0)
    ahead = [compact]
    behind = []
    for direction, held in ((1, ahead), (-1, behind)):
        pairs = [
            (source, (source // group) * group + (source % group + direction) % group)
            for source in range(count)
        ]
        moving = compact
        for _ in range(group // 2 if direction > 0 else (group - 1) // 2):
            moving = lax.ppermute(moving, "curve", pairs)
            held.append(moving)
    near = jnp.concatenate(ahead + behind[::-1], axis=0)
    owner_start = jnp.sum((owner[None, :] < owner[:, None]).astype(jnp.int32), axis=1)
    slot = jnp.arange(bnd_ids.shape[0], dtype=jnp.int32)
    within = jnp.clip(slot - owner_start, 0, BCAP - 1)
    step_of = (member % group - owner % group) % group
    rows = jnp.take(near, step_of * BCAP + within, axis=0)
    ours = (owner // group) == (member // group)
    rows = jnp.where(ours[:, None], rows, jnp.zeros((), rows.dtype))
    return share_rows(rows, owner, member, group)


def attend_heads(picks, count, q_ref, kvt_ref, bkt_ref, bvt_ref, w_ref, o_ref):
    near = len(picks) * BLOCK
    width = near + bkt_ref.shape[2]
    lane = lax.broadcasted_iota(jnp.int32, (1, width), 1)
    live = (lane // BLOCK < count) | (lane >= near)
    rate = LOG2E / q_ref.shape[3] ** 0.5
    contexts = []
    for h in range(HEADS):
        query = q_ref[0, h]
        keys = jnp.concatenate([kvt_ref[p, h] for p in picks] + [bkt_ref[h]], axis=1)
        scores = jnp.dot(query, keys, preferred_element_type=jnp.float32)
        scores = jnp.where(live, scores, -1e30)
        top = jnp.max(scores, axis=1, keepdims=True)
        expo = jnp.exp2((scores - top) * rate)
        total = jnp.sum(expo, axis=1, keepdims=True)
        weights = (expo * (1.0 / total)).astype(jnp.bfloat16)
        values = jnp.concatenate([kvt_ref[p, HEADS + h] for p in picks] + [bvt_ref[h]], axis=1)
        ctx = lax.dot_general(
            values, weights, (((1,), (1,)), ((), ())), preferred_element_type=jnp.float32
        )
        contexts.append(ctx.astype(jnp.bfloat16))
    context = jnp.concatenate(contexts, axis=0)
    mixed = lax.dot_general(
        context, w_ref[...], (((0,), (0,)), ((), ())), preferred_element_type=jnp.float32
    )
    o_ref[0] = mixed.astype(jnp.bfloat16)


def attention_kernel(rel_ref, cnt_ref, q_ref, kvt_ref, bkt_ref, bvt_ref, w_ref, o_ref):
    b = pl.program_id(0)
    count = cnt_ref[b]
    picks = [rel_ref[b * NB + i] for i in range(NB)]
    low = 0
    for high in CLASSES:

        @pl.when((count > low) & (count <= high))
        def _():
            attend_heads(picks[:high], count, q_ref, kvt_ref, bkt_ref, bvt_ref, w_ref, o_ref)

        low = high


def attention(rel, counts, q, kvt, bkt, bvt, w_out):
    nq = q.shape[0]
    nkb = kvt.shape[0]
    head_dim = q.shape[3]
    nbound = bkt.shape[2]
    width = w_out.shape[0]
    grid_spec = pltpu.PrefetchScalarGridSpec(
        num_scalar_prefetch=2,
        grid=(nq,),
        in_specs=[
            pl.BlockSpec((1, HEADS, BLOCK, head_dim), lambda b, r, c: (b, 0, 0, 0)),
            pl.BlockSpec((nkb, 2 * HEADS, head_dim, BLOCK), lambda b, r, c: (0, 0, 0, 0)),
            pl.BlockSpec((HEADS, head_dim, nbound), lambda b, r, c: (0, 0, 0)),
            pl.BlockSpec((HEADS, head_dim, nbound), lambda b, r, c: (0, 0, 0)),
            pl.BlockSpec((width, width), lambda b, r, c: (0, 0)),
        ],
        out_specs=pl.BlockSpec((1, BLOCK, width), lambda b, r, c: (b, 0, 0)),
    )
    return pl.pallas_call(
        attention_kernel,
        grid_spec=grid_spec,
        out_shape=jax.ShapeDtypeStruct((nq, BLOCK, width), jnp.bfloat16),
    )(rel, counts, q, kvt, bkt, bvt, w_out)


def key_tiles(keyvals, width, head_dim):
    rows = keyvals.shape[0]
    keys = keyvals[:, :width].reshape(rows // BLOCK, BLOCK, HEADS, head_dim)
    vals = keyvals[:, width:].reshape(rows // BLOCK, BLOCK, HEADS, head_dim)
    return keys.transpose(0, 2, 3, 1), vals.transpose(0, 2, 3, 1)


def on_device(tokens, w_query, w_keyval, w_out, block_list, block_count, bnd_ids):
    tok_dev, width = tokens.shape
    head_dim = width // HEADS
    nblocks = tok_dev // BLOCK
    member = lax.axis_index("curve")
    queries = jnp.dot(tokens, w_query, preferred_element_type=jnp.float32).astype(jnp.bfloat16)
    queries = queries.reshape(nblocks, BLOCK, HEADS, head_dim).transpose(0, 2, 1, 3)
    pieces = []
    for offset in (-2, -1, 0, 1, 2):
        if offset == 0:
            pieces.append(tokens)
        else:
            pieces.append(from_behind(tokens, "curve", -offset))
    kv_w = w_keyval.reshape(width, 2 * HEADS, head_dim).transpose(1, 2, 0)
    kvt = jnp.zeros((5 * nblocks, 2 * HEADS, head_dim, BLOCK), jnp.bfloat16)
    for index in (2, 0, 1, 3, 4):
        piece = pieces[index]
        part = jnp.einsum(
            "hdc,btc->bhdt",
            kv_w,
            piece.reshape(nblocks, BLOCK, width),
            preferred_element_type=jnp.float32,
        ).astype(jnp.bfloat16)
        kvt = kvt.at[index * nblocks : (index + 1) * nblocks].set(part)
    gathered = boundary_rows(tokens, bnd_ids, member)
    bnd_kv = jnp.dot(gathered, w_keyval, preferred_element_type=jnp.float32).astype(jnp.bfloat16)
    bkt, bvt = key_tiles(bnd_kv, width, head_dim)
    bkt = bkt.transpose(1, 2, 0, 3).reshape(HEADS, head_dim, -1)
    bvt = bvt.transpose(1, 2, 0, 3).reshape(HEADS, head_dim, -1)
    first_block = (member - 2) * nblocks
    rel = jnp.clip(block_list - first_block, 0, 5 * nblocks - 1).reshape(-1).astype(jnp.int32)
    mixed = attention(rel, block_count.astype(jnp.int32), queries, kvt, bkt, bvt, w_out)
    return mixed.reshape(tok_dev, width)


def solution(mesh):
    in_specs = (
        P(("geo", "curve"), None),
        P(),
        P(),
        P(),
        P(("geo", "curve"), None),
        P(("geo", "curve")),
        P("geo"),
    )
    out_specs = P(("geo", "curve"), None)
    return jax.shard_map(
        on_device, mesh=mesh, in_specs=in_specs, out_specs=out_specs, check_vma=False
    )
```

```python
import jax
import jax.numpy as jnp
from jax import lax
from jax.experimental import pallas as pl
from jax.experimental.pallas import tpu as pltpu
from jax.sharding import PartitionSpec as P

HEADS = 8
BLOCK = 128
NB = 12
BCAP = 128
ROW = 8
CLASSES = (4, 8, NB)
LOG2E = 1.4426950408889634


def from_behind(value, axis, steps):
    count = lax.axis_size(axis)
    first, last = (max(0, -steps), min(count, count - steps))
    return lax.ppermute(value, axis, [(source, source + steps) for source in range(first, last)])


def share_rows(rows, owner, member, span):
    count = lax.axis_size("curve")
    while span < count:
        pairs = [(source, source ^ span) for source in range(count) if source ^ span < count]
        other = lax.ppermute(rows, "curve", pairs)
        theirs = (owner // span) == ((member // span) ^ 1)
        rows = jnp.where(theirs[:, None], other, rows)
        span *= 2
    return rows


def boundary_rows(tokens, bnd_ids, member):
    tok_dev = tokens.shape[0]
    count = lax.axis_size("curve")
    group = ROW if count % ROW == 0 else 1
    owner = bnd_ids // tok_dev
    my_start = jnp.sum((owner < member).astype(jnp.int32))
    padded_ids = jnp.concatenate([bnd_ids, jnp.zeros((BCAP,), jnp.int32)])
    my_ids = lax.dynamic_slice_in_dim(padded_ids, my_start, BCAP)
    compact = jnp.take(tokens, jnp.clip(my_ids - member * tok_dev, 0, tok_dev - 1), axis=0)
    pieces = [compact]
    for step in range(1, group):
        pairs = [
            (source, (source // group) * group + (source % group + step) % group)
            for source in range(count)
        ]
        pieces.append(lax.ppermute(compact, "curve", pairs))
    near = jnp.concatenate(pieces, axis=0)
    owner_start = jnp.sum((owner[None, :] < owner[:, None]).astype(jnp.int32), axis=1)
    slot = jnp.arange(bnd_ids.shape[0], dtype=jnp.int32)
    within = jnp.clip(slot - owner_start, 0, BCAP - 1)
    step_of = (member % group - owner % group) % group
    rows = jnp.take(near, step_of * BCAP + within, axis=0)
    ours = (owner // group) == (member // group)
    rows = jnp.where(ours[:, None], rows, jnp.zeros((), rows.dtype))
    return share_rows(rows, owner, member, group)


def attend_heads(picks, count, q_ref, kvt_ref, bkvt_ref, w_ref, o_ref):
    near = len(picks) * BLOCK
    width = near + bkvt_ref.shape[2]
    lane = lax.broadcasted_iota(jnp.int32, (1, width), 1)
    live = (lane // BLOCK < count) | (lane >= near)
    rate = LOG2E / q_ref.shape[3] ** 0.5
    contexts = []
    for h in range(HEADS):
        query = q_ref[0, h]
        keys = jnp.concatenate([kvt_ref[p, h] for p in picks] + [bkvt_ref[h]], axis=1)
        scores = jnp.dot(query, keys, preferred_element_type=jnp.float32)
        scores = jnp.where(live, scores, -1e30)
        top = jnp.max(scores, axis=1, keepdims=True)
        expo = jnp.exp2((scores - top) * rate)
        total = jnp.sum(expo, axis=1, keepdims=True)
        weights = (expo * (1.0 / total)).astype(jnp.bfloat16)
        values = jnp.concatenate([kvt_ref[p, HEADS + h] for p in picks] + [bkvt_ref[HEADS + h]], axis=1)
        ctx = lax.dot_general(
            values, weights, (((1,), (1,)), ((), ())), preferred_element_type=jnp.float32
        )
        contexts.append(ctx.astype(jnp.bfloat16))
    context = jnp.concatenate(contexts, axis=0)
    mixed = lax.dot_general(
        context, w_ref[...], (((0,), (0,)), ((), ())), preferred_element_type=jnp.float32
    )
    o_ref[0] = mixed.astype(jnp.bfloat16)


def attention_kernel(rel_ref, cnt_ref, q_ref, kvt_ref, bkvt_ref, w_ref, o_ref):
    b = pl.program_id(0)
    count = cnt_ref[b]
    picks = [rel_ref[b * NB + i] for i in range(NB)]
    low = 0
    for high in CLASSES:

        @pl.when((count > low) & (count <= high))
        def _():
            attend_heads(picks[:high], count, q_ref, kvt_ref, bkvt_ref, w_ref, o_ref)

        low = high


def attention(rel, counts, q, kvt, bkvt, w_out):
    nq = q.shape[0]
    nkb = kvt.shape[0]
    head_dim = q.shape[3]
    nbound = bkvt.shape[2]
    width = w_out.shape[0]
    grid_spec = pltpu.PrefetchScalarGridSpec(
        num_scalar_prefetch=2,
        grid=(nq,),
        in_specs=[
            pl.BlockSpec((1, HEADS, BLOCK, head_dim), lambda b, r, c: (b, 0, 0, 0)),
            pl.BlockSpec((nkb, 2 * HEADS, head_dim, BLOCK), lambda b, r, c: (0, 0, 0, 0)),
            pl.BlockSpec((2 * HEADS, head_dim, nbound), lambda b, r, c: (0, 0, 0)),
            pl.BlockSpec((width, width), lambda b, r, c: (0, 0)),
        ],
        out_specs=pl.BlockSpec((1, BLOCK, width), lambda b, r, c: (b, 0, 0)),
    )
    return pl.pallas_call(
        attention_kernel,
        grid_spec=grid_spec,
        out_shape=jax.ShapeDtypeStruct((nq, BLOCK, width), jnp.bfloat16),
    )(rel, counts, q, kvt, bkvt, w_out)


def on_device(tokens, w_query, w_keyval, w_out, block_list, block_count, bnd_ids):
    tok_dev, width = tokens.shape
    head_dim = width // HEADS
    nblocks = tok_dev // BLOCK
    member = lax.axis_index("curve")
    queries = jnp.dot(tokens, w_query, preferred_element_type=jnp.float32).astype(jnp.bfloat16)
    queries = queries.reshape(nblocks, BLOCK, HEADS, head_dim).transpose(0, 2, 1, 3)
    pieces = []
    for offset in (-2, -1, 0, 1, 2):
        if offset == 0:
            pieces.append(tokens)
        else:
            pieces.append(from_behind(tokens, "curve", -offset))
    kv_w = w_keyval.reshape(width, 2 * HEADS, head_dim).transpose(1, 2, 0)
    kvt = jnp.zeros((5 * nblocks, 2 * HEADS, head_dim, BLOCK), jnp.bfloat16)
    for index in (2, 0, 1, 3, 4):
        piece = pieces[index]
        part = jnp.einsum(
            "hdc,btc->bhdt",
            kv_w,
            piece.reshape(nblocks, BLOCK, width),
            preferred_element_type=jnp.float32,
        ).astype(jnp.bfloat16)
        kvt = kvt.at[index * nblocks : (index + 1) * nblocks].set(part)
    gathered = boundary_rows(tokens, bnd_ids, member)
    bkvt = jnp.einsum(
        "hdc,nc->hdn", kv_w, gathered, preferred_element_type=jnp.float32
    ).astype(jnp.bfloat16)
    first_block = (member - 2) * nblocks
    rel = jnp.clip(block_list - first_block, 0, 5 * nblocks - 1).reshape(-1).astype(jnp.int32)
    mixed = attention(rel, block_count.astype(jnp.int32), queries, kvt, bkvt, w_out)
    return mixed.reshape(tok_dev, width)


def solution(mesh):
    in_specs = (
        P(("geo", "curve"), None),
        P(),
        P(),
        P(),
        P(("geo", "curve"), None),
        P(("geo", "curve")),
        P("geo"),
    )
    out_specs = P(("geo", "curve"), None)
    return jax.shard_map(
        on_device, mesh=mesh, in_specs=in_specs, out_specs=out_specs, check_vma=False
    )
```

```python
import jax
import jax.numpy as jnp
from jax import lax
from jax.experimental import pallas as pl
from jax.experimental.pallas import tpu as pltpu
from jax.sharding import PartitionSpec as P

HEADS = 8
BLOCK = 128
NB = 12
BCAP = 128
ROW = 8
CLASSES = (4, 8, NB)
LOG2E = 1.4426950408889634


def from_behind(value, axis, steps):
    count = lax.axis_size(axis)
    first, last = (max(0, -steps), min(count, count - steps))
    return lax.ppermute(value, axis, [(source, source + steps) for source in range(first, last)])


def share_rows(rows, owner, member, span):
    count = lax.axis_size("curve")
    while span < count:
        pairs = [(source, source ^ span) for source in range(count) if source ^ span < count]
        other = lax.ppermute(rows, "curve", pairs)
        theirs = (owner // span) == ((member // span) ^ 1)
        rows = jnp.where(theirs[:, None], other, rows)
        span *= 2
    return rows


def boundary_rows(tokens, bnd_ids, member):
    tok_dev = tokens.shape[0]
    count = lax.axis_size("curve")
    group = ROW if count % ROW == 0 else 1
    owner = bnd_ids // tok_dev
    my_start = jnp.sum((owner < member).astype(jnp.int32))
    padded_ids = jnp.concatenate([bnd_ids, jnp.zeros((BCAP,), jnp.int32)])
    my_ids = lax.dynamic_slice_in_dim(padded_ids, my_start, BCAP)
    local = jnp.clip(my_ids - member * tok_dev, 0, tok_dev - 1)
    select = (local[:, None] == jnp.arange(tok_dev, dtype=jnp.int32)[None, :]).astype(tokens.dtype)
    compact = jnp.dot(select, tokens, preferred_element_type=jnp.float32).astype(tokens.dtype)
    pieces = [compact]
    for step in range(1, group):
        pairs = [
            (source, (source // group) * group + (source % group + step) % group)
            for source in range(count)
        ]
        pieces.append(lax.ppermute(compact, "curve", pairs))
    near = jnp.concatenate(pieces, axis=0)
    owner_start = jnp.sum((owner[None, :] < owner[:, None]).astype(jnp.int32), axis=1)
    slot = jnp.arange(bnd_ids.shape[0], dtype=jnp.int32)
    within = jnp.clip(slot - owner_start, 0, BCAP - 1)
    step_of = (member % group - owner % group) % group
    rows = jnp.take(near, step_of * BCAP + within, axis=0)
    ours = (owner // group) == (member // group)
    rows = jnp.where(ours[:, None], rows, jnp.zeros((), rows.dtype))
    return share_rows(rows, owner, member, group)


def attend_heads(picks, count, q_ref, kvt_ref, bkt_ref, bvt_ref, w_ref, o_ref):
    near = len(picks) * BLOCK
    width = near + bkt_ref.shape[2]
    lane = lax.broadcasted_iota(jnp.int32, (1, width), 1)
    live = (lane // BLOCK < count) | (lane >= near)
    rate = LOG2E / q_ref.shape[3] ** 0.5
    contexts = []
    for h in range(HEADS):
        query = q_ref[0, h]
        keys = jnp.concatenate([kvt_ref[p, h] for p in picks] + [bkt_ref[h]], axis=1)
        scores = jnp.dot(query, keys, preferred_element_type=jnp.float32)
        scores = jnp.where(live, scores, -1e30)
        top = jnp.max(scores, axis=1, keepdims=True)
        expo = jnp.exp2((scores - top) * rate)
        total = jnp.sum(expo, axis=1, keepdims=True)
        weights = (expo * (1.0 / total)).astype(jnp.bfloat16)
        values = jnp.concatenate([kvt_ref[p, HEADS + h] for p in picks] + [bvt_ref[h]], axis=1)
        ctx = lax.dot_general(
            values, weights, (((1,), (1,)), ((), ())), preferred_element_type=jnp.float32
        )
        contexts.append(ctx.astype(jnp.bfloat16))
    context = jnp.concatenate(contexts, axis=0)
    mixed = lax.dot_general(
        context, w_ref[...], (((0,), (0,)), ((), ())), preferred_element_type=jnp.float32
    )
    o_ref[0] = mixed.astype(jnp.bfloat16)


def attention_kernel(rel_ref, cnt_ref, q_ref, kvt_ref, bkt_ref, bvt_ref, w_ref, o_ref):
    b = pl.program_id(0)
    count = cnt_ref[b]
    picks = [rel_ref[b * NB + i] for i in range(NB)]
    low = 0
    for high in CLASSES:

        @pl.when((count > low) & (count <= high))
        def _():
            attend_heads(picks[:high], count, q_ref, kvt_ref, bkt_ref, bvt_ref, w_ref, o_ref)

        low = high


def attention(rel, counts, q, kvt, bkt, bvt, w_out):
    nq = q.shape[0]
    nkb = kvt.shape[0]
    head_dim = q.shape[3]
    nbound = bkt.shape[2]
    width = w_out.shape[0]
    grid_spec = pltpu.PrefetchScalarGridSpec(
        num_scalar_prefetch=2,
        grid=(nq,),
        in_specs=[
            pl.BlockSpec((1, HEADS, BLOCK, head_dim), lambda b, r, c: (b, 0, 0, 0)),
            pl.BlockSpec((nkb, 2 * HEADS, head_dim, BLOCK), lambda b, r, c: (0, 0, 0, 0)),
            pl.BlockSpec((HEADS, head_dim, nbound), lambda b, r, c: (0, 0, 0)),
            pl.BlockSpec((HEADS, head_dim, nbound), lambda b, r, c: (0, 0, 0)),
            pl.BlockSpec((width, width), lambda b, r, c: (0, 0)),
        ],
        out_specs=pl.BlockSpec((1, BLOCK, width), lambda b, r, c: (b, 0, 0)),
    )
    return pl.pallas_call(
        attention_kernel,
        grid_spec=grid_spec,
        out_shape=jax.ShapeDtypeStruct((nq, BLOCK, width), jnp.bfloat16),
    )(rel, counts, q, kvt, bkt, bvt, w_out)


def key_tiles(keyvals, width, head_dim):
    rows = keyvals.shape[0]
    keys = keyvals[:, :width].reshape(rows // BLOCK, BLOCK, HEADS, head_dim)
    vals = keyvals[:, width:].reshape(rows // BLOCK, BLOCK, HEADS, head_dim)
    return keys.transpose(0, 2, 3, 1), vals.transpose(0, 2, 3, 1)


def on_device(tokens, w_query, w_keyval, w_out, block_list, block_count, bnd_ids):
    tok_dev, width = tokens.shape
    head_dim = width // HEADS
    nblocks = tok_dev // BLOCK
    member = lax.axis_index("curve")
    queries = jnp.dot(tokens, w_query, preferred_element_type=jnp.float32).astype(jnp.bfloat16)
    queries = queries.reshape(nblocks, BLOCK, HEADS, head_dim).transpose(0, 2, 1, 3)
    pieces = []
    for offset in (-2, -1, 0, 1, 2):
        if offset == 0:
            pieces.append(tokens)
        else:
            pieces.append(from_behind(tokens, "curve", -offset))
    kv_w = w_keyval.reshape(width, 2 * HEADS, head_dim).transpose(1, 2, 0)
    kvt = jnp.zeros((5 * nblocks, 2 * HEADS, head_dim, BLOCK), jnp.bfloat16)
    for index in (2, 0, 1, 3, 4):
        piece = pieces[index]
        part = jnp.einsum(
            "hdc,btc->bhdt",
            kv_w,
            piece.reshape(nblocks, BLOCK, width),
            preferred_element_type=jnp.float32,
        ).astype(jnp.bfloat16)
        kvt = kvt.at[index * nblocks : (index + 1) * nblocks].set(part)
    gathered = boundary_rows(tokens, bnd_ids, member)
    bnd_kv = jnp.dot(gathered, w_keyval, preferred_element_type=jnp.float32).astype(jnp.bfloat16)
    bkt, bvt = key_tiles(bnd_kv, width, head_dim)
    bkt = bkt.transpose(1, 2, 0, 3).reshape(HEADS, head_dim, -1)
    bvt = bvt.transpose(1, 2, 0, 3).reshape(HEADS, head_dim, -1)
    first_block = (member - 2) * nblocks
    rel = jnp.clip(block_list - first_block, 0, 5 * nblocks - 1).reshape(-1).astype(jnp.int32)
    mixed = attention(rel, block_count.astype(jnp.int32), queries, kvt, bkt, bvt, w_out)
    return mixed.reshape(tok_dev, width)


def solution(mesh):
    in_specs = (
        P(("geo", "curve"), None),
        P(),
        P(),
        P(),
        P(("geo", "curve"), None),
        P(("geo", "curve")),
        P("geo"),
    )
    out_specs = P(("geo", "curve"), None)
    return jax.shard_map(
        on_device, mesh=mesh, in_specs=in_specs, out_specs=out_specs, check_vma=False
    )
```

```python
import jax
import jax.numpy as jnp
from jax import lax
from jax.experimental import pallas as pl
from jax.experimental.pallas import tpu as pltpu
from jax.sharding import PartitionSpec as P

HEADS = 8
BLOCK = 128
NB = 12
BCAP = 128
ROW = 8
CLASSES = (3, 6, 9, NB)
LOG2E = 1.4426950408889634


def from_behind(value, axis, steps):
    count = lax.axis_size(axis)
    first, last = (max(0, -steps), min(count, count - steps))
    return lax.ppermute(value, axis, [(source, source + steps) for source in range(first, last)])


def share_rows(rows, owner, member, span):
    count = lax.axis_size("curve")
    while span < count:
        pairs = [(source, source ^ span) for source in range(count) if source ^ span < count]
        other = lax.ppermute(rows, "curve", pairs)
        theirs = (owner // span) == ((member // span) ^ 1)
        rows = jnp.where(theirs[:, None], other, rows)
        span *= 2
    return rows


def boundary_rows(tokens, bnd_ids, member):
    tok_dev = tokens.shape[0]
    count = lax.axis_size("curve")
    group = ROW if count % ROW == 0 else 1
    owner = bnd_ids // tok_dev
    my_start = jnp.sum((owner < member).astype(jnp.int32))
    padded_ids = jnp.concatenate([bnd_ids, jnp.zeros((BCAP,), jnp.int32)])
    my_ids = lax.dynamic_slice_in_dim(padded_ids, my_start, BCAP)
    local = jnp.clip(my_ids - member * tok_dev, 0, tok_dev - 1)
    select = (local[:, None] == jnp.arange(tok_dev, dtype=jnp.int32)[None, :]).astype(tokens.dtype)
    compact = jnp.dot(select, tokens, preferred_element_type=jnp.float32).astype(tokens.dtype)
    pieces = [compact]
    for step in range(1, group):
        pairs = [
            (source, (source // group) * group + (source % group + step) % group)
            for source in range(count)
        ]
        pieces.append(lax.ppermute(compact, "curve", pairs))
    near = jnp.concatenate(pieces, axis=0)
    owner_start = jnp.sum((owner[None, :] < owner[:, None]).astype(jnp.int32), axis=1)
    slot = jnp.arange(bnd_ids.shape[0], dtype=jnp.int32)
    within = jnp.clip(slot - owner_start, 0, BCAP - 1)
    step_of = (member % group - owner % group) % group
    rows = jnp.take(near, step_of * BCAP + within, axis=0)
    ours = (owner // group) == (member // group)
    rows = jnp.where(ours[:, None], rows, jnp.zeros((), rows.dtype))
    return share_rows(rows, owner, member, group)


def attend_heads(picks, count, q_ref, kvt_ref, bkt_ref, bvt_ref, w_ref, o_ref):
    near = len(picks) * BLOCK
    width = near + bkt_ref.shape[2]
    lane = lax.broadcasted_iota(jnp.int32, (1, width), 1)
    live = (lane // BLOCK < count) | (lane >= near)
    rate = LOG2E / q_ref.shape[3] ** 0.5
    contexts = []
    for h in range(HEADS):
        query = q_ref[0, h]
        keys = jnp.concatenate([kvt_ref[p, h] for p in picks] + [bkt_ref[h]], axis=1)
        scores = jnp.dot(query, keys, preferred_element_type=jnp.float32)
        scores = jnp.where(live, scores, -1e30)
        top = jnp.max(scores, axis=1, keepdims=True)
        expo = jnp.exp2((scores - top) * rate)
        total = jnp.sum(expo, axis=1, keepdims=True)
        weights = (expo * (1.0 / total)).astype(jnp.bfloat16)
        values = jnp.concatenate([kvt_ref[p, HEADS + h] for p in picks] + [bvt_ref[h]], axis=1)
        ctx = lax.dot_general(
            values, weights, (((1,), (1,)), ((), ())), preferred_element_type=jnp.float32
        )
        contexts.append(ctx.astype(jnp.bfloat16))
    context = jnp.concatenate(contexts, axis=0)
    mixed = lax.dot_general(
        context, w_ref[...], (((0,), (0,)), ((), ())), preferred_element_type=jnp.float32
    )
    o_ref[0] = mixed.astype(jnp.bfloat16)


def attention_kernel(rel_ref, cnt_ref, q_ref, kvt_ref, bkt_ref, bvt_ref, w_ref, o_ref):
    b = pl.program_id(0)
    count = cnt_ref[b]
    picks = [rel_ref[b * NB + i] for i in range(NB)]
    low = 0
    for high in CLASSES:

        @pl.when((count > low) & (count <= high))
        def _():
            attend_heads(picks[:high], count, q_ref, kvt_ref, bkt_ref, bvt_ref, w_ref, o_ref)

        low = high


def attention(rel, counts, q, kvt, bkt, bvt, w_out):
    nq = q.shape[0]
    nkb = kvt.shape[0]
    head_dim = q.shape[3]
    nbound = bkt.shape[2]
    width = w_out.shape[0]
    grid_spec = pltpu.PrefetchScalarGridSpec(
        num_scalar_prefetch=2,
        grid=(nq,),
        in_specs=[
            pl.BlockSpec((1, HEADS, BLOCK, head_dim), lambda b, r, c: (b, 0, 0, 0)),
            pl.BlockSpec((nkb, 2 * HEADS, head_dim, BLOCK), lambda b, r, c: (0, 0, 0, 0)),
            pl.BlockSpec((HEADS, head_dim, nbound), lambda b, r, c: (0, 0, 0)),
            pl.BlockSpec((HEADS, head_dim, nbound), lambda b, r, c: (0, 0, 0)),
            pl.BlockSpec((width, width), lambda b, r, c: (0, 0)),
        ],
        out_specs=pl.BlockSpec((1, BLOCK, width), lambda b, r, c: (b, 0, 0)),
    )
    return pl.pallas_call(
        attention_kernel,
        grid_spec=grid_spec,
        out_shape=jax.ShapeDtypeStruct((nq, BLOCK, width), jnp.bfloat16),
    )(rel, counts, q, kvt, bkt, bvt, w_out)


def key_tiles(keyvals, width, head_dim):
    rows = keyvals.shape[0]
    keys = keyvals[:, :width].reshape(rows // BLOCK, BLOCK, HEADS, head_dim)
    vals = keyvals[:, width:].reshape(rows // BLOCK, BLOCK, HEADS, head_dim)
    return keys.transpose(0, 2, 3, 1), vals.transpose(0, 2, 3, 1)


def on_device(tokens, w_query, w_keyval, w_out, block_list, block_count, bnd_ids):
    tok_dev, width = tokens.shape
    head_dim = width // HEADS
    nblocks = tok_dev // BLOCK
    member = lax.axis_index("curve")
    queries = jnp.dot(tokens, w_query, preferred_element_type=jnp.float32).astype(jnp.bfloat16)
    queries = queries.reshape(nblocks, BLOCK, HEADS, head_dim).transpose(0, 2, 1, 3)
    pieces = []
    for offset in (-2, -1, 0, 1, 2):
        if offset == 0:
            pieces.append(tokens)
        else:
            pieces.append(from_behind(tokens, "curve", -offset))
    kv_w = w_keyval.reshape(width, 2 * HEADS, head_dim).transpose(1, 2, 0)
    kvt = jnp.zeros((5 * nblocks, 2 * HEADS, head_dim, BLOCK), jnp.bfloat16)
    for index in (2, 0, 1, 3, 4):
        piece = pieces[index]
        part = jnp.einsum(
            "hdc,btc->bhdt",
            kv_w,
            piece.reshape(nblocks, BLOCK, width),
            preferred_element_type=jnp.float32,
        ).astype(jnp.bfloat16)
        kvt = kvt.at[index * nblocks : (index + 1) * nblocks].set(part)
    gathered = boundary_rows(tokens, bnd_ids, member)
    bnd_kv = jnp.dot(gathered, w_keyval, preferred_element_type=jnp.float32).astype(jnp.bfloat16)
    bkt, bvt = key_tiles(bnd_kv, width, head_dim)
    bkt = bkt.transpose(1, 2, 0, 3).reshape(HEADS, head_dim, -1)
    bvt = bvt.transpose(1, 2, 0, 3).reshape(HEADS, head_dim, -1)
    first_block = (member - 2) * nblocks
    rel = jnp.clip(block_list - first_block, 0, 5 * nblocks - 1).reshape(-1).astype(jnp.int32)
    mixed = attention(rel, block_count.astype(jnp.int32), queries, kvt, bkt, bvt, w_out)
    return mixed.reshape(tok_dev, width)


def solution(mesh):
    in_specs = (
        P(("geo", "curve"), None),
        P(),
        P(),
        P(),
        P(("geo", "curve"), None),
        P(("geo", "curve")),
        P("geo"),
    )
    out_specs = P(("geo", "curve"), None)
    return jax.shard_map(
        on_device, mesh=mesh, in_specs=in_specs, out_specs=out_specs, check_vma=False
    )
```

```python
import jax
import jax.numpy as jnp
from jax import lax
from jax.experimental import pallas as pl
from jax.experimental.pallas import tpu as pltpu
from jax.sharding import PartitionSpec as P

HEADS = 8
BLOCK = 128
NB = 12
BCAP = 128
ROW = 8
CLASSES = (4, 8, NB)
LOG2E = 1.4426950408889634


def from_behind(value, axis, steps):
    count = lax.axis_size(axis)
    first, last = (max(0, -steps), min(count, count - steps))
    return lax.ppermute(value, axis, [(source, source + steps) for source in range(first, last)])


def share_rows(rows, owner, member, span):
    count = lax.axis_size("curve")
    while span < count:
        pairs = [(source, source ^ span) for source in range(count) if source ^ span < count]
        other = lax.ppermute(rows, "curve", pairs)
        theirs = (owner // span) == ((member // span) ^ 1)
        rows = jnp.where(theirs[:, None], other, rows)
        span *= 2
    return rows


def boundary_rows(tokens, bnd_ids, member):
    tok_dev = tokens.shape[0]
    count = lax.axis_size("curve")
    group = ROW if count % ROW == 0 else 1
    owner = bnd_ids // tok_dev
    my_start = jnp.sum((owner < member).astype(jnp.int32))
    padded_ids = jnp.concatenate([bnd_ids, jnp.zeros((BCAP,), jnp.int32)])
    my_ids = lax.dynamic_slice_in_dim(padded_ids, my_start, BCAP)
    local = jnp.clip(my_ids - member * tok_dev, 0, tok_dev - 1)
    select = (local[:, None] == jnp.arange(tok_dev, dtype=jnp.int32)[None, :]).astype(tokens.dtype)
    compact = jnp.dot(select, tokens, preferred_element_type=jnp.float32).astype(tokens.dtype)
    pieces = [compact]
    for step in range(1, group):
        pairs = [
            (source, (source // group) * group + (source % group + step) % group)
            for source in range(count)
        ]
        pieces.append(lax.ppermute(compact, "curve", pairs))
    near = jnp.concatenate(pieces, axis=0)
    owner_start = jnp.sum((owner[None, :] < owner[:, None]).astype(jnp.int32), axis=1)
    slot = jnp.arange(bnd_ids.shape[0], dtype=jnp.int32)
    within = jnp.clip(slot - owner_start, 0, BCAP - 1)
    step_of = (member % group - owner % group) % group
    rows = jnp.take(near, step_of * BCAP + within, axis=0)
    ours = (owner // group) == (member // group)
    rows = jnp.where(ours[:, None], rows, jnp.zeros((), rows.dtype))
    return share_rows(rows, owner, member, group)


def attend_heads(picks, count, q_ref, kvt_ref, bkvt_ref, w_ref, o_ref):
    near = len(picks) * BLOCK
    width = near + bkvt_ref.shape[2]
    lane = lax.broadcasted_iota(jnp.int32, (1, width), 1)
    live = (lane // BLOCK < count) | (lane >= near)
    rate = LOG2E / q_ref.shape[3] ** 0.5
    contexts = []
    for h in range(HEADS):
        query = q_ref[0, h]
        keys = jnp.concatenate([kvt_ref[p, h] for p in picks] + [bkvt_ref[h]], axis=1)
        scores = jnp.dot(query, keys, preferred_element_type=jnp.float32)
        scores = jnp.where(live, scores, -1e30)
        top = jnp.max(scores, axis=1, keepdims=True)
        expo = jnp.exp2((scores - top) * rate)
        total = jnp.sum(expo, axis=1, keepdims=True)
        weights = (expo * (1.0 / total)).astype(jnp.bfloat16)
        values = jnp.concatenate([kvt_ref[p, HEADS + h] for p in picks] + [bkvt_ref[HEADS + h]], axis=1)
        ctx = lax.dot_general(
            values, weights, (((1,), (1,)), ((), ())), preferred_element_type=jnp.float32
        )
        contexts.append(ctx.astype(jnp.bfloat16))
    context = jnp.concatenate(contexts, axis=0)
    mixed = lax.dot_general(
        context, w_ref[...], (((0,), (0,)), ((), ())), preferred_element_type=jnp.float32
    )
    o_ref[0] = mixed.astype(jnp.bfloat16)


def attention_kernel(rel_ref, cnt_ref, q_ref, kvt_ref, bkvt_ref, w_ref, o_ref):
    b = pl.program_id(0)
    count = cnt_ref[b]
    picks = [rel_ref[b * NB + i] for i in range(NB)]
    low = 0
    for high in CLASSES:

        @pl.when((count > low) & (count <= high))
        def _():
            attend_heads(picks[:high], count, q_ref, kvt_ref, bkvt_ref, w_ref, o_ref)

        low = high


def attention(rel, counts, q, kvt, bkvt, w_out):
    nq = q.shape[0]
    nkb = kvt.shape[0]
    head_dim = q.shape[3]
    nbound = bkvt.shape[2]
    width = w_out.shape[0]
    grid_spec = pltpu.PrefetchScalarGridSpec(
        num_scalar_prefetch=2,
        grid=(nq,),
        in_specs=[
            pl.BlockSpec((1, HEADS, BLOCK, head_dim), lambda b, r, c: (b, 0, 0, 0)),
            pl.BlockSpec((nkb, 2 * HEADS, head_dim, BLOCK), lambda b, r, c: (0, 0, 0, 0)),
            pl.BlockSpec((2 * HEADS, head_dim, nbound), lambda b, r, c: (0, 0, 0)),
            pl.BlockSpec((width, width), lambda b, r, c: (0, 0)),
        ],
        out_specs=pl.BlockSpec((1, BLOCK, width), lambda b, r, c: (b, 0, 0)),
    )
    return pl.pallas_call(
        attention_kernel,
        grid_spec=grid_spec,
        out_shape=jax.ShapeDtypeStruct((nq, BLOCK, width), jnp.bfloat16),
    )(rel, counts, q, kvt, bkvt, w_out)


def on_device(tokens, w_query, w_keyval, w_out, block_list, block_count, bnd_ids):
    tok_dev, width = tokens.shape
    head_dim = width // HEADS
    nblocks = tok_dev // BLOCK
    member = lax.axis_index("curve")
    queries = jnp.dot(tokens, w_query, preferred_element_type=jnp.float32).astype(jnp.bfloat16)
    queries = queries.reshape(nblocks, BLOCK, HEADS, head_dim).transpose(0, 2, 1, 3)
    pieces = []
    for offset in (-2, -1, 0, 1, 2):
        if offset == 0:
            pieces.append(tokens)
        else:
            pieces.append(from_behind(tokens, "curve", -offset))
    kv_w = w_keyval.reshape(width, 2 * HEADS, head_dim).transpose(1, 2, 0)
    kvt = jnp.zeros((5 * nblocks, 2 * HEADS, head_dim, BLOCK), jnp.bfloat16)
    for index in (2, 0, 1, 3, 4):
        piece = pieces[index]
        part = jnp.einsum(
            "hdc,btc->bhdt",
            kv_w,
            piece.reshape(nblocks, BLOCK, width),
            preferred_element_type=jnp.float32,
        ).astype(jnp.bfloat16)
        kvt = kvt.at[index * nblocks : (index + 1) * nblocks].set(part)
    gathered = boundary_rows(tokens, bnd_ids, member)
    bkvt = jnp.einsum(
        "hdc,nc->hdn", kv_w, gathered, preferred_element_type=jnp.float32
    ).astype(jnp.bfloat16)
    first_block = (member - 2) * nblocks
    rel = jnp.clip(block_list - first_block, 0, 5 * nblocks - 1).reshape(-1).astype(jnp.int32)
    mixed = attention(rel, block_count.astype(jnp.int32), queries, kvt, bkvt, w_out)
    return mixed.reshape(tok_dev, width)


def solution(mesh):
    in_specs = (
        P(("geo", "curve"), None),
        P(),
        P(),
        P(),
        P(("geo", "curve"), None),
        P(("geo", "curve")),
        P("geo"),
    )
    out_specs = P(("geo", "curve"), None)
    return jax.shard_map(
        on_device, mesh=mesh, in_specs=in_specs, out_specs=out_specs, check_vma=False
    )
```

```python
import jax
import jax.numpy as jnp
from jax import lax
from jax.experimental import pallas as pl
from jax.experimental.pallas import tpu as pltpu
from jax.sharding import PartitionSpec as P

HEADS = 8
BLOCK = 128
NB = 12
BCAP = 128
ROW = 8
CLASSES = (4, 8, NB)
LOG2E = 1.4426950408889634


def from_behind(value, axis, steps):
    count = lax.axis_size(axis)
    first, last = (max(0, -steps), min(count, count - steps))
    return lax.ppermute(value, axis, [(source, source + steps) for source in range(first, last)])


def share_rows(rows, owner, member, span):
    count = lax.axis_size("curve")
    while span < count:
        pairs = [(source, source ^ span) for source in range(count) if source ^ span < count]
        other = lax.ppermute(rows, "curve", pairs)
        theirs = (owner // span) == ((member // span) ^ 1)
        rows = jnp.where(theirs[:, None], other, rows)
        span *= 2
    return rows


def boundary_rows(tokens, bnd_ids, member):
    tok_dev = tokens.shape[0]
    count = lax.axis_size("curve")
    group = ROW if count % ROW == 0 else 1
    owner = bnd_ids // tok_dev
    my_start = jnp.sum((owner < member).astype(jnp.int32))
    padded_ids = jnp.concatenate([bnd_ids, jnp.zeros((BCAP,), jnp.int32)])
    my_ids = lax.dynamic_slice_in_dim(padded_ids, my_start, BCAP)
    local = jnp.clip(my_ids - member * tok_dev, 0, tok_dev - 1)
    select = (local[:, None] == jnp.arange(tok_dev, dtype=jnp.int32)[None, :]).astype(tokens.dtype)
    compact = jnp.dot(select, tokens, preferred_element_type=jnp.float32).astype(tokens.dtype)
    pieces = [compact]
    for step in range(1, group):
        pairs = [
            (source, (source // group) * group + (source % group + step) % group)
            for source in range(count)
        ]
        pieces.append(lax.ppermute(compact, "curve", pairs))
    near = jnp.concatenate(pieces, axis=0)
    owner_start = jnp.sum((owner[None, :] < owner[:, None]).astype(jnp.int32), axis=1)
    slot = jnp.arange(bnd_ids.shape[0], dtype=jnp.int32)
    within = jnp.clip(slot - owner_start, 0, BCAP - 1)
    step_of = (member % group - owner % group) % group
    rows = jnp.take(near, step_of * BCAP + within, axis=0)
    ours = (owner // group) == (member // group)
    rows = jnp.where(ours[:, None], rows, jnp.zeros((), rows.dtype))
    return share_rows(rows, owner, member, group)


def attend_heads(picks, count, q_ref, kvt_ref, bkvt_ref, w_ref, o_ref):
    near = len(picks) * BLOCK
    width = near + bkvt_ref.shape[2]
    lane = lax.broadcasted_iota(jnp.int32, (1, width), 1)
    live = (lane // BLOCK < count) | (lane >= near)
    rate = LOG2E / q_ref.shape[3] ** 0.5
    contexts = []
    for h in range(HEADS):
        query = q_ref[0, h]
        keys = jnp.concatenate([kvt_ref[p, h] for p in picks] + [bkvt_ref[h]], axis=1)
        scores = jnp.dot(query, keys, preferred_element_type=jnp.float32)
        scores = jnp.where(live, scores, -1e30)
        top = jnp.max(scores, axis=1, keepdims=True)
        expo = jnp.exp2((scores - top) * rate)
        total = jnp.sum(expo, axis=1, keepdims=True)
        weights = (expo * (1.0 / total)).astype(jnp.bfloat16)
        values = jnp.concatenate([kvt_ref[p, HEADS + h] for p in picks] + [bkvt_ref[HEADS + h]], axis=1)
        ctx = lax.dot_general(
            values, weights, (((1,), (1,)), ((), ())), preferred_element_type=jnp.float32
        )
        contexts.append(ctx.astype(jnp.bfloat16))
    context = jnp.concatenate(contexts, axis=0)
    mixed = lax.dot_general(
        context, w_ref[...], (((0,), (0,)), ((), ())), preferred_element_type=jnp.float32
    )
    o_ref[0] = mixed.astype(jnp.bfloat16)


def attention_kernel(rel_ref, cnt_ref, q_ref, kvt_ref, bkvt_ref, w_ref, o_ref):
    b = pl.program_id(0)
    count = cnt_ref[b]
    picks = [rel_ref[b * NB + i] for i in range(NB)]
    low = 0
    for high in CLASSES:

        @pl.when((count > low) & (count <= high))
        def _():
            attend_heads(picks[:high], count, q_ref, kvt_ref, bkvt_ref, w_ref, o_ref)

        low = high


def attention(rel, counts, q, kvt, bkvt, w_out):
    nq = q.shape[0]
    nkb = kvt.shape[0]
    head_dim = q.shape[3]
    nbound = bkvt.shape[2]
    width = w_out.shape[0]
    grid_spec = pltpu.PrefetchScalarGridSpec(
        num_scalar_prefetch=2,
        grid=(nq,),
        in_specs=[
            pl.BlockSpec((1, HEADS, BLOCK, head_dim), lambda b, r, c: (b, 0, 0, 0)),
            pl.BlockSpec((nkb, 2 * HEADS, head_dim, BLOCK), lambda b, r, c: (0, 0, 0, 0)),
            pl.BlockSpec((2 * HEADS, head_dim, nbound), lambda b, r, c: (0, 0, 0)),
            pl.BlockSpec((width, width), lambda b, r, c: (0, 0)),
        ],
        out_specs=pl.BlockSpec((1, BLOCK, width), lambda b, r, c: (b, 0, 0)),
    )
    return pl.pallas_call(
        attention_kernel,
        grid_spec=grid_spec,
        out_shape=jax.ShapeDtypeStruct((nq, BLOCK, width), jnp.bfloat16),
    )(rel, counts, q, kvt, bkvt, w_out)


def on_device(tokens, w_query, w_keyval, w_out, block_list, block_count, bnd_ids):
    tok_dev, width = tokens.shape
    head_dim = width // HEADS
    nblocks = tok_dev // BLOCK
    member = lax.axis_index("curve")
    queries = jnp.dot(tokens, w_query, preferred_element_type=jnp.float32).astype(jnp.bfloat16)
    queries = queries.reshape(nblocks, BLOCK, HEADS, head_dim).transpose(0, 2, 1, 3)
    pieces = []
    for offset in (-2, -1, 0, 1, 2):
        if offset == 0:
            pieces.append(tokens)
        else:
            pieces.append(from_behind(tokens, "curve", -offset))
    kv_w = w_keyval.reshape(width, 2 * HEADS, head_dim).transpose(1, 2, 0)
    gathered = boundary_rows(tokens, bnd_ids, member)
    bkvt = jnp.einsum(
        "hdc,nc->hdn", kv_w, gathered, preferred_element_type=jnp.float32
    ).astype(jnp.bfloat16)
    bkvt, pieces[0] = lax.optimization_barrier((bkvt, pieces[0]))
    kvt = jnp.zeros((5 * nblocks, 2 * HEADS, head_dim, BLOCK), jnp.bfloat16)
    for index in (2, 0, 1, 3, 4):
        piece = pieces[index]
        part = jnp.einsum(
            "hdc,btc->bhdt",
            kv_w,
            piece.reshape(nblocks, BLOCK, width),
            preferred_element_type=jnp.float32,
        ).astype(jnp.bfloat16)
        kvt = kvt.at[index * nblocks : (index + 1) * nblocks].set(part)
    first_block = (member - 2) * nblocks
    rel = jnp.clip(block_list - first_block, 0, 5 * nblocks - 1).reshape(-1).astype(jnp.int32)
    mixed = attention(rel, block_count.astype(jnp.int32), queries, kvt, bkvt, w_out)
    return mixed.reshape(tok_dev, width)


def solution(mesh):
    in_specs = (
        P(("geo", "curve"), None),
        P(),
        P(),
        P(),
        P(("geo", "curve"), None),
        P(("geo", "curve")),
        P("geo"),
    )
    out_specs = P(("geo", "curve"), None)
    return jax.shard_map(
        on_device, mesh=mesh, in_specs=in_specs, out_specs=out_specs, check_vma=False
    )
```

```python
import jax
import jax.numpy as jnp
from jax import lax
from jax.experimental import pallas as pl
from jax.experimental.pallas import tpu as pltpu
from jax.sharding import PartitionSpec as P

HEADS = 8
BLOCK = 128
NB = 12
BCAP = 128
ROW = 8
CLASSES = (4, 8, NB)
LOG2E = 1.4426950408889634


def from_behind(value, axis, steps):
    count = lax.axis_size(axis)
    first, last = (max(0, -steps), min(count, count - steps))
    return lax.ppermute(value, axis, [(source, source + steps) for source in range(first, last)])


def share_rows(rows, owner, member, span):
    count = lax.axis_size("curve")
    while span < count:
        pairs = [(source, source ^ span) for source in range(count) if source ^ span < count]
        other = lax.ppermute(rows, "curve", pairs)
        theirs = (owner // span) == ((member // span) ^ 1)
        rows = jnp.where(theirs[:, None], other, rows)
        span *= 2
    return rows


def boundary_rows(tokens, bnd_ids, member):
    tok_dev = tokens.shape[0]
    count = lax.axis_size("curve")
    group = ROW if count % ROW == 0 else 1
    owner = bnd_ids // tok_dev
    my_start = jnp.sum((owner < member).astype(jnp.int32))
    padded_ids = jnp.concatenate([bnd_ids, jnp.zeros((BCAP,), jnp.int32)])
    my_ids = lax.dynamic_slice_in_dim(padded_ids, my_start, BCAP)
    local = jnp.clip(my_ids - member * tok_dev, 0, tok_dev - 1)
    select = (local[:, None] == jnp.arange(tok_dev, dtype=jnp.int32)[None, :]).astype(tokens.dtype)
    compact = jnp.dot(select, tokens, preferred_element_type=jnp.float32).astype(tokens.dtype)
    pieces = [compact]
    for step in range(1, group):
        pairs = [
            (source, (source // group) * group + (source % group + step) % group)
            for source in range(count)
        ]
        pieces.append(lax.ppermute(compact, "curve", pairs))
    near = jnp.concatenate(pieces, axis=0)
    owner_start = jnp.sum((owner[None, :] < owner[:, None]).astype(jnp.int32), axis=1)
    slot = jnp.arange(bnd_ids.shape[0], dtype=jnp.int32)
    within = jnp.clip(slot - owner_start, 0, BCAP - 1)
    step_of = (member % group - owner % group) % group
    rows = jnp.take(near, step_of * BCAP + within, axis=0)
    ours = (owner // group) == (member // group)
    rows = jnp.where(ours[:, None], rows, jnp.zeros((), rows.dtype))
    return share_rows(rows, owner, member, group)


def attend_heads(picks, count, q_ref, kvt_ref, bkvt_ref, w_ref, o_ref):
    near = len(picks) * BLOCK
    width = near + bkvt_ref.shape[2]
    lane = lax.broadcasted_iota(jnp.int32, (1, width), 1)
    live = (lane // BLOCK < count) | (lane >= near)
    rate = LOG2E / q_ref.shape[3] ** 0.5
    contexts = []
    for h in range(HEADS):
        query = q_ref[0, h]
        keys = jnp.concatenate([kvt_ref[p, h] for p in picks] + [bkvt_ref[h]], axis=1)
        scores = jnp.dot(query, keys, preferred_element_type=jnp.float32)
        scores = jnp.where(live, scores, -1e30)
        top = jnp.max(scores, axis=1, keepdims=True)
        expo = jnp.exp2((scores - top) * rate)
        total = jnp.sum(expo, axis=1, keepdims=True)
        weights = (expo * (1.0 / total)).astype(jnp.bfloat16)
        values = jnp.concatenate([kvt_ref[p, HEADS + h] for p in picks] + [bkvt_ref[HEADS + h]], axis=1)
        ctx = lax.dot_general(
            values, weights, (((1,), (1,)), ((), ())), preferred_element_type=jnp.float32
        )
        contexts.append(ctx.astype(jnp.bfloat16))
    context = jnp.concatenate(contexts, axis=0)
    mixed = lax.dot_general(
        context, w_ref[...], (((0,), (0,)), ((), ())), preferred_element_type=jnp.float32
    )
    o_ref[0] = mixed.astype(jnp.bfloat16)


def attention_kernel(rel_ref, cnt_ref, q_ref, kvt_ref, bkvt_ref, w_ref, o_ref):
    b = pl.program_id(0)
    count = cnt_ref[b]
    picks = [rel_ref[b * NB + i] for i in range(NB)]
    low = 0
    for high in CLASSES:

        @pl.when((count > low) & (count <= high))
        def _():
            attend_heads(picks[:high], count, q_ref, kvt_ref, bkvt_ref, w_ref, o_ref)

        low = high


def attention(rel, counts, q, kvt, bkvt, w_out):
    nq = q.shape[0]
    nkb = kvt.shape[0]
    head_dim = q.shape[3]
    nbound = bkvt.shape[2]
    width = w_out.shape[0]
    grid_spec = pltpu.PrefetchScalarGridSpec(
        num_scalar_prefetch=2,
        grid=(nq,),
        in_specs=[
            pl.BlockSpec((1, HEADS, BLOCK, head_dim), lambda b, r, c: (b, 0, 0, 0)),
            pl.BlockSpec((nkb, 2 * HEADS, head_dim, BLOCK), lambda b, r, c: (0, 0, 0, 0)),
            pl.BlockSpec((2 * HEADS, head_dim, nbound), lambda b, r, c: (0, 0, 0)),
            pl.BlockSpec((width, width), lambda b, r, c: (0, 0)),
        ],
        out_specs=pl.BlockSpec((1, BLOCK, width), lambda b, r, c: (b, 0, 0)),
    )
    return pl.pallas_call(
        attention_kernel,
        grid_spec=grid_spec,
        out_shape=jax.ShapeDtypeStruct((nq, BLOCK, width), jnp.bfloat16),
    )(rel, counts, q, kvt, bkvt, w_out)


def on_device(tokens, w_query, w_keyval, w_out, block_list, block_count, bnd_ids):
    tok_dev, width = tokens.shape
    head_dim = width // HEADS
    nblocks = tok_dev // BLOCK
    member = lax.axis_index("curve")
    queries = jnp.dot(tokens, w_query, preferred_element_type=jnp.float32).astype(jnp.bfloat16)
    queries = queries.reshape(nblocks, BLOCK, HEADS, head_dim).transpose(0, 2, 1, 3)
    pieces = []
    for offset in (-2, -1, 0, 1, 2):
        if offset == 0:
            pieces.append(tokens)
        else:
            pieces.append(from_behind(tokens, "curve", -offset))
    kv_w = w_keyval.reshape(width, 2 * HEADS, head_dim).transpose(1, 2, 0)
    gathered = boundary_rows(tokens, bnd_ids, member)
    bkvt = jnp.einsum(
        "hdc,nc->hdn", kv_w, gathered, preferred_element_type=jnp.float32
    ).astype(jnp.bfloat16)
    bkvt, pieces[3] = lax.optimization_barrier((bkvt, pieces[3]))
    kvt = jnp.zeros((5 * nblocks, 2 * HEADS, head_dim, BLOCK), jnp.bfloat16)
    for index in (2, 0, 1, 3, 4):
        piece = pieces[index]
        part = jnp.einsum(
            "hdc,btc->bhdt",
            kv_w,
            piece.reshape(nblocks, BLOCK, width),
            preferred_element_type=jnp.float32,
        ).astype(jnp.bfloat16)
        kvt = kvt.at[index * nblocks : (index + 1) * nblocks].set(part)
    first_block = (member - 2) * nblocks
    rel = jnp.clip(block_list - first_block, 0, 5 * nblocks - 1).reshape(-1).astype(jnp.int32)
    mixed = attention(rel, block_count.astype(jnp.int32), queries, kvt, bkvt, w_out)
    return mixed.reshape(tok_dev, width)


def solution(mesh):
    in_specs = (
        P(("geo", "curve"), None),
        P(),
        P(),
        P(),
        P(("geo", "curve"), None),
        P(("geo", "curve")),
        P("geo"),
    )
    out_specs = P(("geo", "curve"), None)
    return jax.shard_map(
        on_device, mesh=mesh, in_specs=in_specs, out_specs=out_specs, check_vma=False
    )
```

```python
import jax
import jax.numpy as jnp
from jax import lax
from jax.experimental import pallas as pl
from jax.experimental.pallas import tpu as pltpu
from jax.sharding import PartitionSpec as P

HEADS = 8
BLOCK = 128
NB = 12
BCAP = 128
ROW = 8
CLASSES = (4, 8, 10, NB)
LOG2E = 1.4426950408889634


def from_behind(value, axis, steps):
    count = lax.axis_size(axis)
    first, last = (max(0, -steps), min(count, count - steps))
    return lax.ppermute(value, axis, [(source, source + steps) for source in range(first, last)])


def share_rows(rows, owner, member, span):
    count = lax.axis_size("curve")
    while span < count:
        pairs = [(source, source ^ span) for source in range(count) if source ^ span < count]
        other = lax.ppermute(rows, "curve", pairs)
        theirs = (owner // span) == ((member // span) ^ 1)
        rows = jnp.where(theirs[:, None], other, rows)
        span *= 2
    return rows


def boundary_rows(tokens, bnd_ids, member):
    tok_dev = tokens.shape[0]
    count = lax.axis_size("curve")
    group = ROW if count % ROW == 0 else 1
    owner = bnd_ids // tok_dev
    my_start = jnp.sum((owner < member).astype(jnp.int32))
    padded_ids = jnp.concatenate([bnd_ids, jnp.zeros((BCAP,), jnp.int32)])
    my_ids = lax.dynamic_slice_in_dim(padded_ids, my_start, BCAP)
    local = jnp.clip(my_ids - member * tok_dev, 0, tok_dev - 1)
    select = (local[:, None] == jnp.arange(tok_dev, dtype=jnp.int32)[None, :]).astype(tokens.dtype)
    compact = jnp.dot(select, tokens, preferred_element_type=jnp.float32).astype(tokens.dtype)
    pieces = [compact]
    for step in range(1, group):
        pairs = [
            (source, (source // group) * group + (source % group + step) % group)
            for source in range(count)
        ]
        pieces.append(lax.ppermute(compact, "curve", pairs))
    near = jnp.concatenate(pieces, axis=0)
    owner_start = jnp.sum((owner[None, :] < owner[:, None]).astype(jnp.int32), axis=1)
    slot = jnp.arange(bnd_ids.shape[0], dtype=jnp.int32)
    within = jnp.clip(slot - owner_start, 0, BCAP - 1)
    step_of = (member % group - owner % group) % group
    rows = jnp.take(near, step_of * BCAP + within, axis=0)
    ours = (owner // group) == (member // group)
    rows = jnp.where(ours[:, None], rows, jnp.zeros((), rows.dtype))
    return share_rows(rows, owner, member, group)


def attend_heads(picks, count, q_ref, kvt_ref, bkvt_ref, w_ref, o_ref):
    near = len(picks) * BLOCK
    width = near + bkvt_ref.shape[2]
    lane = lax.broadcasted_iota(jnp.int32, (1, width), 1)
    live = (lane // BLOCK < count) | (lane >= near)
    rate = LOG2E / q_ref.shape[3] ** 0.5
    contexts = []
    for h in range(HEADS):
        query = q_ref[0, h]
        keys = jnp.concatenate([kvt_ref[p, h] for p in picks] + [bkvt_ref[h]], axis=1)
        scores = jnp.dot(query, keys, preferred_element_type=jnp.float32)
        scores = jnp.where(live, scores, -1e30)
        top = jnp.max(scores, axis=1, keepdims=True)
        expo = jnp.exp2((scores - top) * rate)
        total = jnp.sum(expo, axis=1, keepdims=True)
        weights = (expo * (1.0 / total)).astype(jnp.bfloat16)
        values = jnp.concatenate([kvt_ref[p, HEADS + h] for p in picks] + [bkvt_ref[HEADS + h]], axis=1)
        ctx = lax.dot_general(
            values, weights, (((1,), (1,)), ((), ())), preferred_element_type=jnp.float32
        )
        contexts.append(ctx.astype(jnp.bfloat16))
    context = jnp.concatenate(contexts, axis=0)
    mixed = lax.dot_general(
        context, w_ref[...], (((0,), (0,)), ((), ())), preferred_element_type=jnp.float32
    )
    o_ref[0] = mixed.astype(jnp.bfloat16)


def attention_kernel(rel_ref, cnt_ref, q_ref, kvt_ref, bkvt_ref, w_ref, o_ref):
    b = pl.program_id(0)
    count = cnt_ref[b]
    picks = [rel_ref[b * NB + i] for i in range(NB)]
    low = 0
    for high in CLASSES:

        @pl.when((count > low) & (count <= high))
        def _():
            attend_heads(picks[:high], count, q_ref, kvt_ref, bkvt_ref, w_ref, o_ref)

        low = high


def attention(rel, counts, q, kvt, bkvt, w_out):
    nq = q.shape[0]
    nkb = kvt.shape[0]
    head_dim = q.shape[3]
    nbound = bkvt.shape[2]
    width = w_out.shape[0]
    grid_spec = pltpu.PrefetchScalarGridSpec(
        num_scalar_prefetch=2,
        grid=(nq,),
        in_specs=[
            pl.BlockSpec((1, HEADS, BLOCK, head_dim), lambda b, r, c: (b, 0, 0, 0)),
            pl.BlockSpec((nkb, 2 * HEADS, head_dim, BLOCK), lambda b, r, c: (0, 0, 0, 0)),
            pl.BlockSpec((2 * HEADS, head_dim, nbound), lambda b, r, c: (0, 0, 0)),
            pl.BlockSpec((width, width), lambda b, r, c: (0, 0)),
        ],
        out_specs=pl.BlockSpec((1, BLOCK, width), lambda b, r, c: (b, 0, 0)),
    )
    return pl.pallas_call(
        attention_kernel,
        grid_spec=grid_spec,
        out_shape=jax.ShapeDtypeStruct((nq, BLOCK, width), jnp.bfloat16),
    )(rel, counts, q, kvt, bkvt, w_out)


def on_device(tokens, w_query, w_keyval, w_out, block_list, block_count, bnd_ids):
    tok_dev, width = tokens.shape
    head_dim = width // HEADS
    nblocks = tok_dev // BLOCK
    member = lax.axis_index("curve")
    queries = jnp.dot(tokens, w_query, preferred_element_type=jnp.float32).astype(jnp.bfloat16)
    queries = queries.reshape(nblocks, BLOCK, HEADS, head_dim).transpose(0, 2, 1, 3)
    pieces = []
    for offset in (-2, -1, 0, 1, 2):
        if offset == 0:
            pieces.append(tokens)
        else:
            pieces.append(from_behind(tokens, "curve", -offset))
    kv_w = w_keyval.reshape(width, 2 * HEADS, head_dim).transpose(1, 2, 0)
    kvt = jnp.zeros((5 * nblocks, 2 * HEADS, head_dim, BLOCK), jnp.bfloat16)
    for index in (2, 0, 1, 3, 4):
        piece = pieces[index]
        part = jnp.einsum(
            "hdc,btc->bhdt",
            kv_w,
            piece.reshape(nblocks, BLOCK, width),
            preferred_element_type=jnp.float32,
        ).astype(jnp.bfloat16)
        kvt = kvt.at[index * nblocks : (index + 1) * nblocks].set(part)
    gathered = boundary_rows(tokens, bnd_ids, member)
    bkvt = jnp.einsum(
        "hdc,nc->hdn", kv_w, gathered, preferred_element_type=jnp.float32
    ).astype(jnp.bfloat16)
    first_block = (member - 2) * nblocks
    rel = jnp.clip(block_list - first_block, 0, 5 * nblocks - 1).reshape(-1).astype(jnp.int32)
    mixed = attention(rel, block_count.astype(jnp.int32), queries, kvt, bkvt, w_out)
    return mixed.reshape(tok_dev, width)


def solution(mesh):
    in_specs = (
        P(("geo", "curve"), None),
        P(),
        P(),
        P(),
        P(("geo", "curve"), None),
        P(("geo", "curve")),
        P("geo"),
    )
    out_specs = P(("geo", "curve"), None)
    return jax.shard_map(
        on_device, mesh=mesh, in_specs=in_specs, out_specs=out_specs, check_vma=False
    )
```
